512 devices in a mesh: leaf: 128 (over z, y, core), grp: 4 (over x).
Axes of the slice: x: 4, y: 4, z: 16, core: 2. Of those that a mesh axis runs over, the one named last changes fastest.
Arguments:
- sources: bfloat16 [16, 2097152], P(None, ('leaf', 'grp')), may hold values from -6 to 6
- points: float32 [3, 2097152], P(None, ('leaf', 'grp')), may hold values from -3 to 83
- near_offsets: int32 [32768, 6], P(('leaf', 'grp')), may hold values from -16 to 16, as said below
- far_offsets: int32 [32768, 8], P(('leaf', 'grp')), may hold values from -32 to 32, as said below
- source_basis: bfloat16 [32768, 2048], P(('leaf', 'grp')), may hold values from -0.75 to 0.75
- target_basis: bfloat16 [32768, 2048], P(('leaf', 'grp')), may hold values from -1 to 1
- leaf_coupling: bfloat16 [32768, 8, 1024], P(('leaf', 'grp')), may hold values from -0.375 to 0.375
- leaf_up: bfloat16 [32768, 1024], P(('leaf', 'grp')), may hold values from -0.125 to 0.125
- leaf_down: bfloat16 [32768, 1024], P(('leaf', 'grp')), may hold values from -1 to 1
- tree_up: bfloat16 [512, 3, 1024], P(('leaf', 'grp')), may hold values from -1 to 1, as said below
- tree_down: bfloat16 [512, 3, 1024], P(('leaf', 'grp')), may hold values from -1 to 1, as said below
- tree_coupling: bfloat16 [512, 4, 4, 1024], P(('leaf', 'grp')), may hold values from -1 to 1, as said below
Outputs:
- product: float32 [16, 2097152], P(None, ('leaf', 'grp'))
The draws below stay inside these ranges and needn't reach their ends.
Inputs may be any that keep to these rules, and one draw needn't show every extreme that they name: `near_offsets`: each row holds 6 distinct offsets, one of them 0 and one of them 16 or -16; the first leaf of each device subtree (i % 64 = 0) holds -16, the last holds 16. `far_offsets`: each row holds 8 distinct offsets of magnitude 16 + 1 to 32, one of them of magnitude 32; the first leaf of each device subtree holds -32, the last holds 32. tree_up[d, s] is the same for all d with equal d // 2**s. tree_down[d, s] is the same for all d with equal d // 2**s. tree_coupling[d, s] is the same for all d with equal d // 2**s.
All inputs are finite; a program needn't handle non-finite values.
Results may differ from the reference program's by a relative error of at most 0.0012.
Values sent between devices are 32-bit elements; how exact they have to be, the bound alone decides.
No kernel may reach another device: no remote copies, remote signals or barrier semaphores. Data moves between devices by JAX's collectives and lax.ppermute only.
A program may use at most 128 MiB of HBM per device.

```python
import jax
import jax.numpy as jnp
from jax import lax

CLUSTER = 64
RANK = 32
RHS = 16
LEAVES_DEV = 64
NEAR_REACH = 16
NEAR_BLOCKS = 6
FAR_REACH = 32
FAR_BLOCKS = 8
TOP_LEVELS = 3
ROOTS = 512
LEAVES = 32768
NODES = 2097152


spacing = 0.08


period = 1001


def offset_rows(key, inner_reach, outer_reach, pick_count, with_zero):
    row_count = LEAVES
    sign_bits = jax.random.randint(jax.random.fold_in(key, 1), (row_count, 1), 0, 2, dtype=jnp.int32)
    position = (jnp.arange(row_count, dtype=jnp.int32) % LEAVES_DEV)[:, None]
    sign_bits = jnp.where(position == 0, 0, jnp.where(position == LEAVES_DEV - 1, 1, sign_bits))
    forced = (sign_bits * 2 - 1) * outer_reach
    magnitudes = jnp.arange(inner_reach + 1, outer_reach, dtype=jnp.int32)
    shared_pool = jnp.broadcast_to(jnp.concatenate([-magnitudes, magnitudes])[None, :], (row_count, 2 * (outer_reach - inner_reach - 1)))
    candidates = jnp.concatenate([shared_pool, -forced], axis=1)
    pool_width = candidates.shape[1]
    scores = jax.random.randint(jax.random.fold_in(key, 2), (row_count, pool_width), 0, 1 << 20, dtype=jnp.int32) * pool_width + jnp.arange(pool_width, dtype=jnp.int32)[None, :]
    ranking = jnp.argsort(scores, axis=1)[:, :pick_count]
    chosen = jnp.take_along_axis(candidates, ranking, axis=1)
    pieces = [forced, chosen]
    if with_zero:
        pieces = [jnp.zeros((row_count, 1), jnp.int32)] + pieces
    joined = jnp.concatenate(pieces, axis=1)
    column_total = joined.shape[1]
    shuffle = jax.random.randint(jax.random.fold_in(key, 3), (row_count, column_total), 0, 1 << 20, dtype=jnp.int32) * column_total + jnp.arange(column_total, dtype=jnp.int32)[None, :]
    return jnp.take_along_axis(joined, jnp.argsort(shuffle, axis=1), axis=1)


def draw_near_offsets(key, part):
    return offset_rows(jax.random.fold_in(key, 15), 0, NEAR_REACH, NEAR_BLOCKS - 2, True)


def draw_far_offsets(key, part):
    return offset_rows(jax.random.fold_in(key, 16), NEAR_REACH, FAR_REACH, FAR_BLOCKS - 1, False)


def draw_points(key, part):
    own_key = jax.random.fold_in(key, 14)
    leaf_of = jnp.arange(NODES, dtype=jnp.int32) // CLUSTER
    along = (leaf_of % period).astype(jnp.float32) * spacing
    jitter = jnp.clip(0.6 * jax.random.normal(own_key, (3, NODES), jnp.float32), -3.0, 3.0)
    lifted = jnp.zeros((3, NODES), jnp.float32).at[0].set(along)
    return jitter + lifted


def tree_copies(key, level_total, members, spread):
    pieces = []
    for tree_level in range(level_total):
        group_size = 2 ** tree_level
        sub_key = jax.random.fold_in(key, tree_level)
        block_shape = (ROOTS // group_size, members, RANK * RANK)
        values = jnp.clip(jax.random.normal(sub_key, block_shape, jnp.float32), -2.5, 2.5) * spread
        pieces.append(jnp.repeat(values, group_size, axis=0))
    return jnp.stack(pieces, axis=1)


def draw_tree_up(key, part):
    return tree_copies(jax.random.fold_in(key, 11), TOP_LEVELS, 1, (2.0 * RANK) ** (-0.5)).reshape(ROOTS, TOP_LEVELS, RANK * RANK).astype(jnp.bfloat16)


def draw_tree_down(key, part):
    return tree_copies(jax.random.fold_in(key, 12), TOP_LEVELS, 1, (1.0 * RANK) ** (-0.5)).reshape(ROOTS, TOP_LEVELS, RANK * RANK).astype(jnp.bfloat16)


def draw_tree_coupling(key, part):
    return tree_copies(jax.random.fold_in(key, 13), TOP_LEVELS + 1, 4, (4.0 * RANK) ** (-0.5)).astype(jnp.bfloat16)


def block_scale(rng, extent, cuts, least, top_value):
    factor_of = 1.0
    for axis_at, blocks in cuts:
        heights = jax.random.uniform(jax.random.fold_in(jax.random.fold_in(rng, 6), axis_at), (blocks,), jnp.float32, least / len(cuts), top_value / len(cuts))
        factor_of = factor_of * jnp.repeat(jnp.exp(heights), extent[axis_at] // blocks).reshape((-1,) + (1,) * (len(extent) - 1 - axis_at))
    return factor_of


def gaussian(rng, shape, deviation, reach, shards=(), held_as=jnp.bfloat16):
    values = jax.random.normal(rng, shape, jnp.float32) * deviation
    if len(shards) > 0:
        values = block_scale(rng, shape, shards, -0.22, 0.18) * values
    return jnp.clip(values, min=-reach, max=reach).astype(held_as)


def setup_inputs(seed: int = 0) -> dict:
    arg_keys = jax.random.split(jax.random.key(seed), 13)
    sources = gaussian(arg_keys[0], (RHS, NODES), 1.0, 6.0, ((1, 512),))
    points = draw_points(jax.random.fold_in(arg_keys[12], 71), 0)
    near_offsets = draw_near_offsets(jax.random.fold_in(arg_keys[12], 71), 0)
    far_offsets = draw_far_offsets(jax.random.fold_in(arg_keys[12], 71), 0)
    source_basis = gaussian(arg_keys[4], (LEAVES, CLUSTER * RANK), CLUSTER ** -0.5, 0.75, ((0, 512),))
    target_basis = gaussian(arg_keys[5], (LEAVES, RANK * CLUSTER), RANK ** -0.5, 1.0, ((0, 512),))
    leaf_coupling = gaussian(arg_keys[6], (LEAVES, FAR_BLOCKS, RANK * RANK), (FAR_BLOCKS * RANK) ** -0.5, 0.375, ((0, 512),))
    leaf_up = gaussian(arg_keys[7], (LEAVES, RANK * RANK), (LEAVES_DEV * RANK) ** -0.5, 0.125, ((0, 512),))
    leaf_down = gaussian(arg_keys[8], (LEAVES, RANK * RANK), RANK ** -0.5, 1.0, ((0, 512),))
    tree_up = draw_tree_up(jax.random.fold_in(arg_keys[12], 71), 0)
    tree_down = draw_tree_down(jax.random.fold_in(arg_keys[12], 71), 0)
    tree_coupling = draw_tree_coupling(jax.random.fold_in(arg_keys[12], 71), 0)
    return {"sources": sources, "points": points, "near_offsets": near_offsets, "far_offsets": far_offsets, "source_basis": source_basis, "target_basis": target_basis, "leaf_coupling": leaf_coupling, "leaf_up": leaf_up, "leaf_down": leaf_down, "tree_up": tree_up, "tree_down": tree_down, "tree_coupling": tree_coupling}


amplitude = 0.15
length_scale = 1.0
nugget = 0.5
partner_steps = (-3, -2, 2, 3)
highest = lax.Precision.HIGHEST

def matern_term(extended, target_points, slot_offsets):
    leaf_count = target_points.shape[1]
    column_count = extended.shape[0] - 3
    source_leaf = jnp.arange(leaf_count, dtype=jnp.int32) + NEAR_REACH + slot_offsets.astype(jnp.int32)
    chosen = jnp.take(extended, source_leaf, axis=1)
    squared = jnp.zeros((leaf_count, CLUSTER, CLUSTER), jnp.float32)
    for component in range(3):
        separation = chosen[column_count + component][:, :, None] - target_points[component][:, None, :]
        squared = squared + separation * separation
    kernel = lax.optimization_barrier((amplitude * jnp.exp(-jnp.sqrt(squared) / length_scale)).astype(jnp.bfloat16)).astype(jnp.float32)
    values = chosen[:column_count]
    return jnp.einsum('rla,lab->rlb', values, kernel, precision=highest)

def reference(sources, points, near_offsets, far_offsets, source_basis, target_basis, leaf_coupling, leaf_up, leaf_down, tree_up, tree_down, tree_coupling):
    leaf_values = sources.astype(jnp.float32).reshape(RHS, LEAVES, CLUSTER)
    point_blocks = points.reshape(3, LEAVES, CLUSTER)
    extended = jnp.pad(jnp.concatenate([leaf_values, point_blocks], axis=0), ((0, 0), (NEAR_REACH, NEAR_REACH), (0, 0)))

    def near_block(block_index):
        first_leaf = block_index * LEAVES_DEV
        window = lax.dynamic_slice_in_dim(extended, first_leaf, LEAVES_DEV + 2 * NEAR_REACH, 1)
        targets = lax.dynamic_slice_in_dim(point_blocks, first_leaf, LEAVES_DEV, 1)
        offsets = lax.dynamic_slice_in_dim(near_offsets, first_leaf, LEAVES_DEV, 0)
        own_values = lax.dynamic_slice_in_dim(leaf_values, first_leaf, LEAVES_DEV, 1)
        summed = nugget * own_values
        for near_slot in range(NEAR_BLOCKS):
            summed = summed + matern_term(window, targets, offsets[:, near_slot])
        return summed
    near_parts = lax.map(near_block, jnp.arange(ROOTS, dtype=jnp.int32))
    near_sum = jnp.transpose(near_parts, (1, 0, 2, 3)).reshape(RHS, LEAVES, CLUSTER)
    leaf_coefficients = jnp.einsum('rla,lak->lrk', leaf_values, source_basis.astype(jnp.float32).reshape(LEAVES, CLUSTER, RANK), precision=highest)
    rimmed = jnp.pad(leaf_coefficients.reshape(LEAVES, RHS * RANK), ((FAR_REACH, FAR_REACH), (0, 0)))
    couplings = leaf_coupling.astype(jnp.float32).reshape(LEAVES, FAR_BLOCKS, RANK, RANK)
    base_index = jnp.arange(LEAVES, dtype=jnp.int32) + FAR_REACH
    leaf_far = jnp.zeros((LEAVES, RHS, RANK), jnp.float32)
    for far_slot in range(FAR_BLOCKS):
        partner = jnp.take(rimmed, base_index + far_offsets[:, far_slot].astype(jnp.int32), axis=0).reshape(LEAVES, RHS, RANK)
        leaf_far = leaf_far + jnp.einsum('lrk,lkq->lrq', partner, couplings[:, far_slot], precision=highest)
    root_coefficients = jnp.einsum('dlrk,dlkq->drq', leaf_coefficients.reshape(ROOTS, LEAVES_DEV, RHS, RANK), leaf_up.astype(jnp.float32).reshape(ROOTS, LEAVES_DEV, RANK, RANK), precision=highest)
    level_coefficients = [root_coefficients]
    current = root_coefficients
    for tree_level in range(TOP_LEVELS):
        group_size = 2 ** tree_level
        matrices = tree_up[::group_size, tree_level].astype(jnp.float32).reshape(-1, RANK, RANK)
        lifted = jnp.einsum('grk,gkq->grq', current, matrices, precision=highest)
        current = lifted.reshape(-1, 2, RHS, RANK).sum(axis=1)
        level_coefficients.append(current)
    level_terms = []
    for tree_level in range(TOP_LEVELS + 1):
        group_size = 2 ** tree_level
        node_count = ROOTS // group_size
        matrices = tree_coupling[::group_size, tree_level].astype(jnp.float32).reshape(node_count, 4, RANK, RANK)
        padded = jnp.pad(level_coefficients[tree_level], ((3, 3), (0, 0), (0, 0)))
        summed = jnp.zeros((node_count, RHS, RANK), jnp.float32)
        for partner_slot, partner_step in enumerate(partner_steps):
            shifted = padded[3 + partner_step:3 + partner_step + node_count]
            summed = summed + jnp.einsum('grk,gkq->grq', shifted, matrices[:, partner_slot], precision=highest)
        level_terms.append(summed)
    downward = level_terms[TOP_LEVELS]
    for tree_level in reversed(range(TOP_LEVELS)):
        group_size = 2 ** tree_level
        matrices = tree_down[::group_size, tree_level].astype(jnp.float32).reshape(-1, RANK, RANK)
        downward = level_terms[tree_level] + jnp.einsum('grk,gkq->grq', jnp.repeat(downward, 2, axis=0), matrices, precision=highest)
    from_root = jnp.einsum('drk,dlkq->dlrq', downward, leaf_down.astype(jnp.float32).reshape(ROOTS, LEAVES_DEV, RANK, RANK), precision=highest)
    leaf_field = leaf_far + from_root.reshape(LEAVES, RHS, RANK)
    far_out = jnp.einsum('lrk,lka->rla', leaf_field, target_basis.astype(jnp.float32).reshape(LEAVES, RANK, CLUSTER), precision=highest)
    return (near_sum + far_out).reshape(RHS, NODES)
```

```python
import jax
import jax.numpy as jnp
from jax import lax
from jax.sharding import PartitionSpec as P

CLUSTER = 64
RANK = 32
RHS = 16
NEAR_REACH = 16
NEAR_BLOCKS = 6
FAR_REACH = 32
FAR_BLOCKS = 8
TOP_LEVELS = 3


amplitude = 0.15
length_scale = 1.0
nugget = 0.5
partner_steps = (-3, -2, 2, 3)
highest = lax.Precision.HIGHEST
AXES = ("leaf", "grp")


def device_count():
    return lax.axis_size("leaf") * lax.axis_size("grp")


def swap_with(value, mask):
    n = device_count()
    return lax.ppermute(value, AXES, [(i, i ^ mask) for i in range(n)])


def receive_from(value, step):
    n = device_count()
    return lax.ppermute(value, AXES, [(s, s - step) for s in range(n) if 0 <= s - step < n])


def matern_term(extended, target_points, slot_offsets):
    leaf_count = target_points.shape[1]
    column_count = extended.shape[0] - 3
    source_leaf = jnp.arange(leaf_count, dtype=jnp.int32) + NEAR_REACH + slot_offsets
    chosen = jnp.take(extended, source_leaf, axis=1)
    squared = jnp.zeros((leaf_count, CLUSTER, CLUSTER), jnp.float32)
    for component in range(3):
        separation = (
            chosen[column_count + component][:, :, None] - target_points[component][:, None, :]
        )
        squared = squared + separation * separation
    kernel = (amplitude * jnp.exp(-jnp.sqrt(squared) / length_scale)).astype(jnp.bfloat16)
    values = chosen[:column_count].astype(jnp.bfloat16)
    return jnp.einsum("rla,lab->rlb", values, kernel, preferred_element_type=jnp.float32)


def mm(a, b):
    return jnp.matmul(a, b, precision=highest, preferred_element_type=jnp.float32)


def ordered(bit, own, other):
    return jnp.where(bit == 0, jnp.concatenate([own, other]), jnp.concatenate([other, own]))


def tree_field(root_coefficients, tree_up, tree_down, tree_coupling, me):
    up = tree_up[0].astype(jnp.float32).reshape(TOP_LEVELS, RANK, RANK)
    down = tree_down[0].astype(jnp.float32).reshape(TOP_LEVELS, RANK, RANK)
    cross = tree_coupling[0].astype(jnp.float32).reshape(TOP_LEVELS + 1, 4, RANK, RANK)
    eye = jnp.eye(RANK, dtype=jnp.float32)
    lift1 = up[0]
    lift2 = mm(lift1, up[1])
    lift3 = mm(lift2, up[2])
    lifts = jnp.stack([eye, lift1, lift2, lift3])
    push1 = down[0]
    push2 = mm(down[1], push1)
    push3 = mm(down[2], push2)
    pushes = jnp.stack([eye, push1, push2, push3])
    weights = jnp.einsum("sqkp,spm->sqkm", cross, pushes, precision=highest)

    p = jnp.einsum("rk,skq->srq", root_coefficients, lifts, precision=highest)

    bit0 = me & 1
    bit1 = (me >> 1) & 1
    bit2 = (me >> 2) & 1
    got1 = swap_with(p, 1)
    pairs0 = ordered(bit0, p[0:1], got1[0:1])
    coef1 = p[1] + got1[1]
    part2 = p[2] + got1[2]
    part3 = p[3] + got1[3]
    got2 = swap_with(jnp.concatenate([pairs0, coef1[None], part2[None], part3[None]]), 2)
    quads0 = ordered(bit1, pairs0, got2[0:2])
    pairs1 = ordered(bit1, coef1[None], got2[2:3])
    coef2 = part2 + got2[3]
    part3 = part3 + got2[4]
    got3 = swap_with(jnp.concatenate([quads0, pairs1, coef2[None], part3[None]]), 4)
    octs0 = ordered(bit2, quads0, got3[0:4])
    quads1 = ordered(bit2, pairs1, got3[4:6])
    pairs2 = ordered(bit2, coef2[None], got3[6:7])
    coef3 = (part3 + got3[7])[None]

    node = 8
    ahead1 = receive_from(jnp.concatenate([octs0[0:3], quads1[0:3], pairs2]), node)
    behind1 = receive_from(jnp.concatenate([octs0[5:8], quads1[1:4], pairs2]), -node)
    ahead2 = receive_from(jnp.concatenate([pairs2[0:1], coef3]), 2 * node)
    behind2 = receive_from(jnp.concatenate([pairs2[1:2], coef3]), -2 * node)
    ahead3 = receive_from(coef3, 3 * node)
    behind3 = receive_from(coef3, -3 * node)

    window0 = jnp.concatenate([behind1[0:3], octs0, ahead1[0:3]])
    window1 = jnp.concatenate([behind1[3:6], quads1, ahead1[3:6]])
    window2 = jnp.concatenate([behind2[0:1], behind1[6:8], pairs2, ahead1[6:8], ahead2[0:1]])
    steps = jnp.array(partner_steps, dtype=jnp.int32) + 3
    chosen0 = jnp.take(window0, (me & 7) + steps, axis=0, mode="clip")
    chosen1 = jnp.take(window1, ((me >> 1) & 3) + steps, axis=0, mode="clip")
    chosen2 = jnp.take(window2, bit2 + steps, axis=0, mode="clip")
    chosen3 = jnp.concatenate([behind3, behind2[1:2], ahead2[1:2], ahead3])
    chosen = jnp.stack([chosen0, chosen1, chosen2, chosen3])
    return jnp.einsum("sqrk,sqkm->rm", chosen, weights, precision=highest)


def local(
    sources,
    points,
    near_offsets,
    far_offsets,
    source_basis,
    target_basis,
    leaf_coupling,
    leaf_up,
    leaf_down,
    tree_up,
    tree_down,
    tree_coupling,
):
    leaf_count = near_offsets.shape[0]
    n = device_count()
    me = lax.axis_index("leaf") * lax.axis_size("grp") + lax.axis_index("grp")
    leaf_values = sources.reshape(RHS, leaf_count, CLUSTER)
    leaf_coefficients = jnp.einsum(
        "rla,lak->lrk",
        leaf_values,
        source_basis.reshape(leaf_count, CLUSTER, RANK),
        preferred_element_type=jnp.float32,
    )
    coef_rows = leaf_coefficients.reshape(leaf_count, RHS * RANK)

    packed = jnp.concatenate([sources.astype(jnp.float32), points], axis=0)
    width = NEAR_REACH * CLUSTER
    to_right = jnp.concatenate(
        [packed[:, -width:].reshape(-1), coef_rows[-FAR_REACH:].reshape(-1)]
    )
    to_left = jnp.concatenate([packed[:, :width].reshape(-1), coef_rows[:FAR_REACH].reshape(-1)])
    from_left = lax.ppermute(to_right, AXES, [(i, i + 1) for i in range(n - 1)])
    from_right = lax.ppermute(to_left, AXES, [(i + 1, i) for i in range(n - 1)])
    split = (RHS + 3) * width
    extended = jnp.concatenate(
        [
            from_left[:split].reshape(RHS + 3, width),
            packed,
            from_right[:split].reshape(RHS + 3, width),
        ],
        axis=1,
    ).reshape(RHS + 3, leaf_count + 2 * NEAR_REACH, CLUSTER)
    rimmed = jnp.concatenate(
        [
            from_left[split:].reshape(FAR_REACH, RHS * RANK),
            coef_rows,
            from_right[split:].reshape(FAR_REACH, RHS * RANK),
        ]
    )

    target_points = points.reshape(3, leaf_count, CLUSTER)
    near_sum = nugget * leaf_values.astype(jnp.float32)
    for near_slot in range(NEAR_BLOCKS):
        near_sum = near_sum + matern_term(extended, target_points, near_offsets[:, near_slot])

    far_index = jnp.arange(leaf_count, dtype=jnp.int32)[:, None] + FAR_REACH + far_offsets
    partner_blocks = jnp.take(rimmed, far_index, axis=0).reshape(leaf_count, FAR_BLOCKS, RHS, RANK)
    leaf_far = jnp.einsum(
        "lfrk,lfkq->lrq",
        partner_blocks,
        leaf_coupling.reshape(leaf_count, FAR_BLOCKS, RANK, RANK),
        precision=highest,
        preferred_element_type=jnp.float32,
    )
    root_coefficients = jnp.einsum(
        "lrk,lkq->rq",
        leaf_coefficients,
        leaf_up.reshape(leaf_count, RANK, RANK),
        precision=highest,
        preferred_element_type=jnp.float32,
    )
    downward = tree_field(root_coefficients, tree_up, tree_down, tree_coupling, me)
    from_root = jnp.einsum(
        "rk,lkq->lrq",
        downward,
        leaf_down.reshape(leaf_count, RANK, RANK),
        precision=highest,
        preferred_element_type=jnp.float32,
    )
    leaf_field = leaf_far + from_root
    far_out = jnp.einsum(
        "lrk,lka->rla",
        leaf_field,
        target_basis.reshape(leaf_count, RANK, CLUSTER),
        precision=highest,
        preferred_element_type=jnp.float32,
    )
    return (near_sum + far_out).reshape(RHS, leaf_count * CLUSTER)


def solution(mesh):
    placed = (
        P(None, AXES),
        P(None, AXES),
        P(AXES, None),
        P(AXES, None),
        P(AXES, None),
        P(AXES, None),
        P(AXES, None, None),
        P(AXES, None),
        P(AXES, None),
        P(AXES, None, None),
        P(AXES, None, None),
        P(AXES, None, None, None),
    )
    return jax.shard_map(
        local, mesh=mesh, in_specs=placed, out_specs=P(None, AXES), check_vma=False
    )
```

```python
import jax
import jax.numpy as jnp
from jax import lax
from jax.sharding import PartitionSpec as P

CLUSTER = 64
RANK = 32
RHS = 16
NEAR_REACH = 16
NEAR_BLOCKS = 6
FAR_REACH = 32
FAR_BLOCKS = 8
TOP_LEVELS = 3


amplitude = 0.15
length_scale = 1.0
nugget = 0.5
partner_steps = (-3, -2, 2, 3)
highest = lax.Precision.HIGHEST
AXES = ("leaf", "grp")


def device_count():
    return lax.axis_size("leaf") * lax.axis_size("grp")


def swap_with(value, mask):
    n = device_count()
    return lax.ppermute(value, AXES, [(i, i ^ mask) for i in range(n)])


def receive_from(value, step):
    n = device_count()
    return lax.ppermute(value, AXES, [(s, s - step) for s in range(n) if 0 <= s - step < n])


def matern_term(extended, target_points, slot_offsets):
    leaf_count = target_points.shape[1]
    column_count = extended.shape[0] - 3
    source_leaf = jnp.arange(leaf_count, dtype=jnp.int32) + NEAR_REACH + slot_offsets
    chosen = jnp.take(extended, source_leaf, axis=1)
    squared = jnp.zeros((leaf_count, CLUSTER, CLUSTER), jnp.float32)
    for component in range(3):
        separation = (
            chosen[column_count + component][:, :, None] - target_points[component][:, None, :]
        )
        squared = squared + separation * separation
    kernel = (amplitude * jnp.exp(-jnp.sqrt(squared) / length_scale)).astype(jnp.bfloat16)
    values = chosen[:column_count].astype(jnp.bfloat16)
    return jnp.einsum("rla,lab->rlb", values, kernel, preferred_element_type=jnp.float32)


def mm(a, b):
    return jnp.matmul(a, b, precision=highest, preferred_element_type=jnp.float32)


def split3(x):
    hi = lax.reduce_precision(x, exponent_bits=8, mantissa_bits=7)
    rest = x - hi
    mid = lax.reduce_precision(rest, exponent_bits=8, mantissa_bits=7)
    lo = rest - mid
    return jnp.stack([hi, mid, lo]).astype(jnp.bfloat16)


def ordered(bit, own, other):
    return jnp.where(bit == 0, jnp.concatenate([own, other]), jnp.concatenate([other, own]))


def tree_field(root_coefficients, tree_up, tree_down, tree_coupling, me):
    up = tree_up[0].astype(jnp.float32).reshape(TOP_LEVELS, RANK, RANK)
    down = tree_down[0].astype(jnp.float32).reshape(TOP_LEVELS, RANK, RANK)
    cross = tree_coupling[0].astype(jnp.float32).reshape(TOP_LEVELS + 1, 4, RANK, RANK)
    eye = jnp.eye(RANK, dtype=jnp.float32)
    lift1 = up[0]
    lift2 = mm(lift1, up[1])
    lift3 = mm(lift2, up[2])
    lifts = jnp.stack([eye, lift1, lift2, lift3])
    push1 = down[0]
    push2 = mm(down[1], push1)
    push3 = mm(down[2], push2)
    pushes = jnp.stack([eye, push1, push2, push3])
    weights = jnp.einsum("sqkp,spm->sqkm", cross, pushes, precision=highest)

    p = jnp.einsum("rk,skq->srq", root_coefficients, lifts, precision=highest)

    bit0 = me & 1
    bit1 = (me >> 1) & 1
    bit2 = (me >> 2) & 1
    got1 = swap_with(p, 1)
    pairs0 = ordered(bit0, p[0:1], got1[0:1])
    coef1 = p[1] + got1[1]
    part2 = p[2] + got1[2]
    part3 = p[3] + got1[3]
    got2 = swap_with(jnp.concatenate([pairs0, coef1[None], part2[None], part3[None]]), 2)
    quads0 = ordered(bit1, pairs0, got2[0:2])
    pairs1 = ordered(bit1, coef1[None], got2[2:3])
    coef2 = part2 + got2[3]
    part3 = part3 + got2[4]
    got3 = swap_with(jnp.concatenate([quads0, pairs1, coef2[None], part3[None]]), 4)
    octs0 = ordered(bit2, quads0, got3[0:4])
    quads1 = ordered(bit2, pairs1, got3[4:6])
    pairs2 = ordered(bit2, coef2[None], got3[6:7])
    coef3 = (part3 + got3[7])[None]

    node = 8
    ahead1 = receive_from(jnp.concatenate([octs0[0:3], quads1[0:3], pairs2, coef3]), node)
    behind1 = receive_from(jnp.concatenate([octs0[5:8], quads1[1:4], pairs2, coef3]), -node)
    ahead2 = receive_from(jnp.concatenate([pairs2[0:1], coef3, ahead1[8:9]]), 2 * node)
    behind2 = receive_from(jnp.concatenate([pairs2[1:2], coef3, behind1[8:9]]), -2 * node)
    ahead3 = ahead2[2:3]
    behind3 = behind2[2:3]

    window0 = jnp.concatenate([behind1[0:3], octs0, ahead1[0:3]])
    window1 = jnp.concatenate([behind1[3:6], quads1, ahead1[3:6]])
    window2 = jnp.concatenate([behind2[0:1], behind1[6:8], pairs2, ahead1[6:8], ahead2[0:1]])
    steps = jnp.array(partner_steps, dtype=jnp.int32) + 3
    chosen0 = jnp.take(window0, (me & 7) + steps, axis=0, mode="clip")
    chosen1 = jnp.take(window1, ((me >> 1) & 3) + steps, axis=0, mode="clip")
    chosen2 = jnp.take(window2, bit2 + steps, axis=0, mode="clip")
    chosen3 = jnp.concatenate([behind3, behind2[1:2], ahead2[1:2], ahead3])
    chosen = jnp.stack([chosen0, chosen1, chosen2, chosen3])
    return jnp.einsum("sqrk,sqkm->rm", chosen, weights, precision=highest)


def local(
    sources,
    points,
    near_offsets,
    far_offsets,
    source_basis,
    target_basis,
    leaf_coupling,
    leaf_up,
    leaf_down,
    tree_up,
    tree_down,
    tree_coupling,
):
    leaf_count = near_offsets.shape[0]
    n = device_count()
    me = lax.axis_index("leaf") * lax.axis_size("grp") + lax.axis_index("grp")
    leaf_values = sources.reshape(RHS, leaf_count, CLUSTER)
    leaf_coefficients = jnp.einsum(
        "rla,lak->lrk",
        leaf_values,
        source_basis.reshape(leaf_count, CLUSTER, RANK),
        preferred_element_type=jnp.float32,
    )
    coef_rows = leaf_coefficients.reshape(leaf_count, RHS * RANK)

    packed = jnp.concatenate([sources.astype(jnp.float32), points], axis=0)
    width = NEAR_REACH * CLUSTER
    to_right = jnp.concatenate(
        [packed[:, -width:].reshape(-1), coef_rows[-FAR_REACH:].reshape(-1)]
    )
    to_left = jnp.concatenate([packed[:, :width].reshape(-1), coef_rows[:FAR_REACH].reshape(-1)])
    from_left = lax.ppermute(to_right, AXES, [(i, i + 1) for i in range(n - 1)])
    from_right = lax.ppermute(to_left, AXES, [(i + 1, i) for i in range(n - 1)])
    split = (RHS + 3) * width
    extended = jnp.concatenate(
        [
            from_left[:split].reshape(RHS + 3, width),
            packed,
            from_right[:split].reshape(RHS + 3, width),
        ],
        axis=1,
    ).reshape(RHS + 3, leaf_count + 2 * NEAR_REACH, CLUSTER)
    rimmed = jnp.concatenate(
        [
            from_left[split:].reshape(FAR_REACH, RHS * RANK),
            coef_rows,
            from_right[split:].reshape(FAR_REACH, RHS * RANK),
        ]
    )

    target_points = points.reshape(3, leaf_count, CLUSTER)
    near_sum = nugget * leaf_values.astype(jnp.float32)
    for near_slot in range(NEAR_BLOCKS):
        near_sum = near_sum + matern_term(extended, target_points, near_offsets[:, near_slot])

    far_index = jnp.arange(leaf_count, dtype=jnp.int32)[:, None] + FAR_REACH + far_offsets
    partner_blocks = jnp.take(rimmed, far_index, axis=0).reshape(leaf_count, FAR_BLOCKS, RHS, RANK)
    leaf_far = jnp.einsum(
        "slfrk,lfkq->lrq",
        split3(partner_blocks),
        leaf_coupling.reshape(leaf_count, FAR_BLOCKS, RANK, RANK),
        preferred_element_type=jnp.float32,
    )
    root_coefficients = jnp.einsum(
        "lrk,lkq->rq",
        leaf_coefficients,
        leaf_up.reshape(leaf_count, RANK, RANK),
        precision=highest,
        preferred_element_type=jnp.float32,
    )
    downward = tree_field(root_coefficients, tree_up, tree_down, tree_coupling, me)
    from_root = jnp.einsum(
        "rk,lkq->lrq",
        downward,
        leaf_down.reshape(leaf_count, RANK, RANK),
        precision=highest,
        preferred_element_type=jnp.float32,
    )
    leaf_field = leaf_far + from_root
    far_out = jnp.einsum(
        "lrk,lka->rla",
        leaf_field,
        target_basis.reshape(leaf_count, RANK, CLUSTER),
        precision=highest,
        preferred_element_type=jnp.float32,
    )
    return (near_sum + far_out).reshape(RHS, leaf_count * CLUSTER)


def solution(mesh):
    placed = (
        P(None, AXES),
        P(None, AXES),
        P(AXES, None),
        P(AXES, None),
        P(AXES, None),
        P(AXES, None),
        P(AXES, None, None),
        P(AXES, None),
        P(AXES, None),
        P(AXES, None, None),
        P(AXES, None, None),
        P(AXES, None, None, None),
    )
    return jax.shard_map(
        local, mesh=mesh, in_specs=placed, out_specs=P(None, AXES), check_vma=False
    )
```

```python
import jax
import jax.numpy as jnp
from jax import lax
from jax.sharding import PartitionSpec as P

CLUSTER = 64
RANK = 32
RHS = 16
NEAR_REACH = 16
NEAR_BLOCKS = 6
FAR_REACH = 32
FAR_BLOCKS = 8
TOP_LEVELS = 3


amplitude = 0.15
length_scale = 1.0
nugget = 0.5
partner_steps = (-3, -2, 2, 3)
highest = lax.Precision.HIGHEST
AXES = ("leaf", "grp")


def device_count():
    return lax.axis_size("leaf") * lax.axis_size("grp")


def swap_with(value, mask):
    n = device_count()
    return lax.ppermute(value, AXES, [(i, i ^ mask) for i in range(n)])


def receive_from(value, step):
    n = device_count()
    return lax.ppermute(value, AXES, [(s, s - step) for s in range(n) if 0 <= s - step < n])


def near_field(extended, target_points, near_offsets, leaf_values):
    leaf_count = target_points.shape[1]
    column_count = extended.shape[0] - 3
    by_leaf = jnp.transpose(extended, (1, 0, 2))
    source_leaf = jnp.arange(leaf_count, dtype=jnp.int32)[:, None] + NEAR_REACH + near_offsets
    chosen = jnp.take(by_leaf, source_leaf, axis=0, mode="clip")
    squared = jnp.zeros((leaf_count, NEAR_BLOCKS, CLUSTER, CLUSTER), jnp.float32)
    for component in range(3):
        separation = (
            chosen[:, :, column_count + component, :, None]
            - target_points[component][:, None, None, :]
        )
        squared = squared + separation * separation
    kernel = (amplitude * jnp.exp(-jnp.sqrt(squared) / length_scale)).astype(jnp.bfloat16)
    values = chosen[:, :, :column_count].astype(jnp.bfloat16)
    near = jnp.einsum("lnra,lnab->rlb", values, kernel, preferred_element_type=jnp.float32)
    return nugget * leaf_values.astype(jnp.float32) + near


def mm(a, b):
    return jnp.matmul(a, b, precision=highest, preferred_element_type=jnp.float32)


def ordered(bit, own, other):
    return jnp.where(bit == 0, jnp.concatenate([own, other]), jnp.concatenate([other, own]))


def tree_field(root_coefficients, tree_up, tree_down, tree_coupling, me):
    up = tree_up[0].astype(jnp.float32).reshape(TOP_LEVELS, RANK, RANK)
    down = tree_down[0].astype(jnp.float32).reshape(TOP_LEVELS, RANK, RANK)
    cross = tree_coupling[0].astype(jnp.float32).reshape(TOP_LEVELS + 1, 4, RANK, RANK)
    eye = jnp.eye(RANK, dtype=jnp.float32)
    lift1 = up[0]
    lift2 = mm(lift1, up[1])
    lift3 = mm(lift2, up[2])
    lifts = jnp.stack([eye, lift1, lift2, lift3])
    push1 = down[0]
    push2 = mm(down[1], push1)
    push3 = mm(down[2], push2)
    pushes = jnp.stack([eye, push1, push2, push3])
    weights = jnp.einsum("sqkp,spm->sqkm", cross, pushes, precision=highest)

    p = jnp.einsum("rk,skq->srq", root_coefficients, lifts, precision=highest)

    bit0 = me & 1
    bit1 = (me >> 1) & 1
    bit2 = (me >> 2) & 1
    got1 = swap_with(p, 1)
    pairs0 = ordered(bit0, p[0:1], got1[0:1])
    coef1 = p[1] + got1[1]
    part2 = p[2] + got1[2]
    part3 = p[3] + got1[3]
    got2 = swap_with(jnp.concatenate([pairs0, coef1[None], part2[None], part3[None]]), 2)
    quads0 = ordered(bit1, pairs0, got2[0:2])
    pairs1 = ordered(bit1, coef1[None], got2[2:3])
    coef2 = part2 + got2[3]
    part3 = part3 + got2[4]
    got3 = swap_with(jnp.concatenate([quads0, pairs1, coef2[None], part3[None]]), 4)
    octs0 = ordered(bit2, quads0, got3[0:4])
    quads1 = ordered(bit2, pairs1, got3[4:6])
    pairs2 = ordered(bit2, coef2[None], got3[6:7])
    coef3 = (part3 + got3[7])[None]

    node = 8
    ahead1 = receive_from(jnp.concatenate([octs0[0:3], quads1[0:3], pairs2, coef3]), node)
    behind1 = receive_from(jnp.concatenate([octs0[5:8], quads1[1:4], pairs2, coef3]), -node)
    ahead2 = receive_from(jnp.concatenate([pairs2[0:1], coef3, ahead1[8:9]]), 2 * node)
    behind2 = receive_from(jnp.concatenate([pairs2[1:2], coef3, behind1[8:9]]), -2 * node)
    ahead3 = ahead2[2:3]
    behind3 = behind2[2:3]

    window0 = jnp.concatenate([behind1[0:3], octs0, ahead1[0:3]])
    window1 = jnp.concatenate([behind1[3:6], quads1, ahead1[3:6]])
    window2 = jnp.concatenate([behind2[0:1], behind1[6:8], pairs2, ahead1[6:8], ahead2[0:1]])
    steps = jnp.array(partner_steps, dtype=jnp.int32) + 3
    chosen0 = jnp.take(window0, (me & 7) + steps, axis=0, mode="clip")
    chosen1 = jnp.take(window1, ((me >> 1) & 3) + steps, axis=0, mode="clip")
    chosen2 = jnp.take(window2, bit2 + steps, axis=0, mode="clip")
    chosen3 = jnp.concatenate([behind3, behind2[1:2], ahead2[1:2], ahead3])
    chosen = jnp.stack([chosen0, chosen1, chosen2, chosen3])
    return jnp.einsum("sqrk,sqkm->rm", chosen, weights, precision=highest)


def local(
    sources,
    points,
    near_offsets,
    far_offsets,
    source_basis,
    target_basis,
    leaf_coupling,
    leaf_up,
    leaf_down,
    tree_up,
    tree_down,
    tree_coupling,
):
    leaf_count = near_offsets.shape[0]
    n = device_count()
    me = lax.axis_index("leaf") * lax.axis_size("grp") + lax.axis_index("grp")
    leaf_values = sources.reshape(RHS, leaf_count, CLUSTER)
    leaf_coefficients = jnp.einsum(
        "rla,lak->lrk",
        leaf_values,
        source_basis.reshape(leaf_count, CLUSTER, RANK),
        preferred_element_type=jnp.float32,
    )
    coef_rows = leaf_coefficients.reshape(leaf_count, RHS * RANK)

    packed = jnp.concatenate([sources.astype(jnp.float32), points], axis=0)
    width = NEAR_REACH * CLUSTER
    to_right = jnp.concatenate(
        [packed[:, -width:].reshape(-1), coef_rows[-FAR_REACH:].reshape(-1)]
    )
    to_left = jnp.concatenate([packed[:, :width].reshape(-1), coef_rows[:FAR_REACH].reshape(-1)])
    from_left = lax.ppermute(to_right, AXES, [(i, i + 1) for i in range(n - 1)])
    from_right = lax.ppermute(to_left, AXES, [(i + 1, i) for i in range(n - 1)])
    split = (RHS + 3) * width
    extended = jnp.concatenate(
        [
            from_left[:split].reshape(RHS + 3, width),
            packed,
            from_right[:split].reshape(RHS + 3, width),
        ],
        axis=1,
    ).reshape(RHS + 3, leaf_count + 2 * NEAR_REACH, CLUSTER)
    rimmed = jnp.concatenate(
        [
            from_left[split:].reshape(FAR_REACH, RHS * RANK),
            coef_rows,
            from_right[split:].reshape(FAR_REACH, RHS * RANK),
        ]
    )

    target_points = points.reshape(3, leaf_count, CLUSTER)
    near_sum = near_field(extended, target_points, near_offsets, leaf_values)

    far_index = jnp.arange(leaf_count, dtype=jnp.int32)[:, None] + FAR_REACH + far_offsets
    partner_blocks = jnp.take(rimmed, far_index, axis=0).reshape(leaf_count, FAR_BLOCKS, RHS, RANK)
    leaf_far = jnp.einsum(
        "lfrk,lfkq->lrq",
        partner_blocks,
        leaf_coupling.reshape(leaf_count, FAR_BLOCKS, RANK, RANK),
        precision=highest,
        preferred_element_type=jnp.float32,
    )
    root_coefficients = jnp.einsum(
        "lrk,lkq->rq",
        leaf_coefficients,
        leaf_up.reshape(leaf_count, RANK, RANK),
        precision=highest,
        preferred_element_type=jnp.float32,
    )
    downward = tree_field(root_coefficients, tree_up, tree_down, tree_coupling, me)
    from_root = jnp.einsum(
        "rk,lkq->lrq",
        downward,
        leaf_down.reshape(leaf_count, RANK, RANK),
        precision=highest,
        preferred_element_type=jnp.float32,
    )
    leaf_field = leaf_far + from_root
    far_out = jnp.einsum(
        "lrk,lka->rla",
        leaf_field,
        target_basis.reshape(leaf_count, RANK, CLUSTER),
        precision=highest,
        preferred_element_type=jnp.float32,
    )
    return (near_sum + far_out).reshape(RHS, leaf_count * CLUSTER)


def solution(mesh):
    placed = (
        P(None, AXES),
        P(None, AXES),
        P(AXES, None),
        P(AXES, None),
        P(AXES, None),
        P(AXES, None),
        P(AXES, None, None),
        P(AXES, None),
        P(AXES, None),
        P(AXES, None, None),
        P(AXES, None, None),
        P(AXES, None, None, None),
    )
    return jax.shard_map(
        local, mesh=mesh, in_specs=placed, out_specs=P(None, AXES), check_vma=False
    )
```

```python
import jax
import jax.numpy as jnp
from jax import lax
from jax.sharding import PartitionSpec as P

CLUSTER = 64
RANK = 32
RHS = 16
NEAR_REACH = 16
NEAR_BLOCKS = 6
FAR_REACH = 32
FAR_BLOCKS = 8
TOP_LEVELS = 3


amplitude = 0.15
length_scale = 1.0
nugget = 0.5
partner_steps = (-3, -2, 2, 3)
highest = lax.Precision.HIGHEST
AXES = ("leaf", "grp")


def device_count():
    return lax.axis_size("leaf") * lax.axis_size("grp")


def swap_with(value, mask):
    n = device_count()
    return lax.ppermute(value, AXES, [(i, i ^ mask) for i in range(n)])


def receive_from(value, step):
    n = device_count()
    return lax.ppermute(value, AXES, [(s, s - step) for s in range(n) if 0 <= s - step < n])


def near_field(extended, target_points, near_offsets, leaf_values):
    leaf_count = target_points.shape[1]
    column_count = extended.shape[0] - 3
    by_leaf = jnp.transpose(extended, (1, 0, 2))
    source_leaf = jnp.arange(leaf_count, dtype=jnp.int32)[:, None] + NEAR_REACH + near_offsets
    chosen = jnp.take(by_leaf, source_leaf, axis=0, mode="clip")
    chosen = jnp.transpose(chosen, (0, 2, 1, 3)).reshape(
        leaf_count, column_count + 3, NEAR_BLOCKS * CLUSTER
    )
    squared = jnp.zeros((leaf_count, CLUSTER, NEAR_BLOCKS * CLUSTER), jnp.float32)
    for component in range(3):
        separation = (
            chosen[:, column_count + component][:, None, :]
            - target_points[component][:, :, None]
        )
        squared = squared + separation * separation
    kernel = (amplitude * jnp.exp(-jnp.sqrt(squared) / length_scale)).astype(jnp.bfloat16)
    values = chosen[:, :column_count].astype(jnp.bfloat16)
    near = jnp.einsum("lrm,lbm->rlb", values, kernel, preferred_element_type=jnp.float32)
    return nugget * leaf_values.astype(jnp.float32) + near


def mm(a, b):
    return jnp.matmul(a, b, precision=highest, preferred_element_type=jnp.float32)


def ordered(bit, own, other):
    return jnp.where(bit == 0, jnp.concatenate([own, other]), jnp.concatenate([other, own]))


def tree_field(root_coefficients, tree_up, tree_down, tree_coupling, me):
    up = tree_up[0].astype(jnp.float32).reshape(TOP_LEVELS, RANK, RANK)
    down = tree_down[0].astype(jnp.float32).reshape(TOP_LEVELS, RANK, RANK)
    cross = tree_coupling[0].astype(jnp.float32).reshape(TOP_LEVELS + 1, 4, RANK, RANK)
    eye = jnp.eye(RANK, dtype=jnp.float32)
    lift1 = up[0]
    lift2 = mm(lift1, up[1])
    lift3 = mm(lift2, up[2])
    lifts = jnp.stack([eye, lift1, lift2, lift3])
    push1 = down[0]
    push2 = mm(down[1], push1)
    push3 = mm(down[2], push2)
    pushes = jnp.stack([eye, push1, push2, push3])
    weights = jnp.einsum("sqkp,spm->sqkm", cross, pushes, precision=highest)

    p = jnp.einsum("rk,skq->srq", root_coefficients, lifts, precision=highest)

    bit0 = me & 1
    bit1 = (me >> 1) & 1
    bit2 = (me >> 2) & 1
    got1 = swap_with(p, 1)
    pairs0 = ordered(bit0, p[0:1], got1[0:1])
    coef1 = p[1] + got1[1]
    part2 = p[2] + got1[2]
    part3 = p[3] + got1[3]
    got2 = swap_with(jnp.concatenate([pairs0, coef1[None], part2[None], part3[None]]), 2)
    quads0 = ordered(bit1, pairs0, got2[0:2])
    pairs1 = ordered(bit1, coef1[None], got2[2:3])
    coef2 = part2 + got2[3]
    part3 = part3 + got2[4]
    got3 = swap_with(jnp.concatenate([quads0, pairs1, coef2[None], part3[None]]), 4)
    octs0 = ordered(bit2, quads0, got3[0:4])
    quads1 = ordered(bit2, pairs1, got3[4:6])
    pairs2 = ordered(bit2, coef2[None], got3[6:7])
    coef3 = (part3 + got3[7])[None]

    node = 8
    ahead1 = receive_from(jnp.concatenate([octs0[0:3], quads1[0:3], pairs2, coef3]), node)
    behind1 = receive_from(jnp.concatenate([octs0[5:8], quads1[1:4], pairs2, coef3]), -node)
    ahead2 = receive_from(jnp.concatenate([pairs2[0:1], coef3, ahead1[8:9]]), 2 * node)
    behind2 = receive_from(jnp.concatenate([pairs2[1:2], coef3, behind1[8:9]]), -2 * node)
    ahead3 = ahead2[2:3]
    behind3 = behind2[2:3]

    window0 = jnp.concatenate([behind1[0:3], octs0, ahead1[0:3]])
    window1 = jnp.concatenate([behind1[3:6], quads1, ahead1[3:6]])
    window2 = jnp.concatenate([behind2[0:1], behind1[6:8], pairs2, ahead1[6:8], ahead2[0:1]])
    steps = jnp.array(partner_steps, dtype=jnp.int32) + 3
    chosen0 = jnp.take(window0, (me & 7) + steps, axis=0, mode="clip")
    chosen1 = jnp.take(window1, ((me >> 1) & 3) + steps, axis=0, mode="clip")
    chosen2 = jnp.take(window2, bit2 + steps, axis=0, mode="clip")
    chosen3 = jnp.concatenate([behind3, behind2[1:2], ahead2[1:2], ahead3])
    chosen = jnp.stack([chosen0, chosen1, chosen2, chosen3])
    return jnp.einsum("sqrk,sqkm->rm", chosen, weights, precision=highest)


def local(
    sources,
    points,
    near_offsets,
    far_offsets,
    source_basis,
    target_basis,
    leaf_coupling,
    leaf_up,
    leaf_down,
    tree_up,
    tree_down,
    tree_coupling,
):
    leaf_count = near_offsets.shape[0]
    n = device_count()
    me = lax.axis_index("leaf") * lax.axis_size("grp") + lax.axis_index("grp")
    leaf_values = sources.reshape(RHS, leaf_count, CLUSTER)
    leaf_coefficients = jnp.einsum(
        "rla,lak->lrk",
        leaf_values,
        source_basis.reshape(leaf_count, CLUSTER, RANK),
        preferred_element_type=jnp.float32,
    )
    coef_rows = leaf_coefficients.reshape(leaf_count, RHS * RANK)

    packed = jnp.concatenate([sources.astype(jnp.float32), points], axis=0)
    width = NEAR_REACH * CLUSTER
    to_right = jnp.concatenate(
        [packed[:, -width:].reshape(-1), coef_rows[-FAR_REACH:].reshape(-1)]
    )
    to_left = jnp.concatenate([packed[:, :width].reshape(-1), coef_rows[:FAR_REACH].reshape(-1)])
    from_left = lax.ppermute(to_right, AXES, [(i, i + 1) for i in range(n - 1)])
    from_right = lax.ppermute(to_left, AXES, [(i + 1, i) for i in range(n - 1)])
    split = (RHS + 3) * width
    extended = jnp.concatenate(
        [
            from_left[:split].reshape(RHS + 3, width),
            packed,
            from_right[:split].reshape(RHS + 3, width),
        ],
        axis=1,
    ).reshape(RHS + 3, leaf_count + 2 * NEAR_REACH, CLUSTER)
    rimmed = jnp.concatenate(
        [
            from_left[split:].reshape(FAR_REACH, RHS * RANK),
            coef_rows,
            from_right[split:].reshape(FAR_REACH, RHS * RANK),
        ]
    )

    target_points = points.reshape(3, leaf_count, CLUSTER)
    near_sum = near_field(extended, target_points, near_offsets, leaf_values)

    far_index = jnp.arange(leaf_count, dtype=jnp.int32)[:, None] + FAR_REACH + far_offsets
    partner_blocks = jnp.take(rimmed, far_index, axis=0).reshape(leaf_count, FAR_BLOCKS, RHS, RANK)
    leaf_far = jnp.einsum(
        "lfrk,lfkq->lrq",
        partner_blocks,
        leaf_coupling.reshape(leaf_count, FAR_BLOCKS, RANK, RANK),
        precision=highest,
        preferred_element_type=jnp.float32,
    )
    root_coefficients = jnp.einsum(
        "lrk,lkq->rq",
        leaf_coefficients,
        leaf_up.reshape(leaf_count, RANK, RANK),
        precision=highest,
        preferred_element_type=jnp.float32,
    )
    downward = tree_field(root_coefficients, tree_up, tree_down, tree_coupling, me)
    from_root = jnp.einsum(
        "rk,lkq->lrq",
        downward,
        leaf_down.reshape(leaf_count, RANK, RANK),
        precision=highest,
        preferred_element_type=jnp.float32,
    )
    leaf_field = leaf_far + from_root
    far_out = jnp.einsum(
        "lrk,lka->rla",
        leaf_field,
        target_basis.reshape(leaf_count, RANK, CLUSTER),
        precision=highest,
        preferred_element_type=jnp.float32,
    )
    return (near_sum + far_out).reshape(RHS, leaf_count * CLUSTER)


def solution(mesh):
    placed = (
        P(None, AXES),
        P(None, AXES),
        P(AXES, None),
        P(AXES, None),
        P(AXES, None),
        P(AXES, None),
        P(AXES, None, None),
        P(AXES, None),
        P(AXES, None),
        P(AXES, None, None),
        P(AXES, None, None),
        P(AXES, None, None, None),
    )
    return jax.shard_map(
        local, mesh=mesh, in_specs=placed, out_specs=P(None, AXES), check_vma=False
    )
```

```python
import jax
import jax.numpy as jnp
from jax import lax
from jax.sharding import PartitionSpec as P

CLUSTER = 64
RANK = 32
RHS = 16
NEAR_REACH = 16
NEAR_BLOCKS = 6
FAR_REACH = 32
FAR_BLOCKS = 8
TOP_LEVELS = 3


amplitude = 0.15
length_scale = 1.0
nugget = 0.5
partner_steps = (-3, -2, 2, 3)
highest = lax.Precision.HIGHEST
AXES = ("leaf", "grp")


def device_count():
    return lax.axis_size("leaf") * lax.axis_size("grp")


def swap_with(value, mask):
    n = device_count()
    return lax.ppermute(value, AXES, [(i, i ^ mask) for i in range(n)])


def receive_from(value, step):
    n = device_count()
    return lax.ppermute(value, AXES, [(s, s - step) for s in range(n) if 0 <= s - step < n])


def near_field(extended, target_points, near_offsets, leaf_values):
    leaf_count = target_points.shape[1]
    column_count = extended.shape[0] - 3
    by_leaf = jnp.transpose(extended, (1, 0, 2))
    base = jnp.arange(leaf_count, dtype=jnp.int32) + NEAR_REACH
    chosen = jnp.concatenate(
        [
            jnp.take(by_leaf, base + near_offsets[:, near_slot], axis=0, mode="clip")
            for near_slot in range(NEAR_BLOCKS)
        ],
        axis=2,
    )
    chosen = jnp.transpose(chosen, (1, 0, 2))
    squared = jnp.zeros((leaf_count, CLUSTER, NEAR_BLOCKS * CLUSTER), jnp.float32)
    for component in range(3):
        separation = (
            chosen[column_count + component][:, None, :] - target_points[component][:, :, None]
        )
        squared = squared + separation * separation
    kernel = (amplitude * jnp.exp(-jnp.sqrt(squared) / length_scale)).astype(jnp.bfloat16)
    values = chosen[:column_count].astype(jnp.bfloat16)
    near = jnp.einsum("rlm,lbm->rlb", values, kernel, preferred_element_type=jnp.float32)
    return nugget * leaf_values.astype(jnp.float32) + near


def mm(a, b):
    return jnp.matmul(a, b, precision=highest, preferred_element_type=jnp.float32)


def ordered(bit, own, other):
    return jnp.where(bit == 0, jnp.concatenate([own, other]), jnp.concatenate([other, own]))


def tree_field(root_coefficients, tree_up, tree_down, tree_coupling, me):
    up = tree_up[0].astype(jnp.float32).reshape(TOP_LEVELS, RANK, RANK)
    down = tree_down[0].astype(jnp.float32).reshape(TOP_LEVELS, RANK, RANK)
    cross = tree_coupling[0].astype(jnp.float32).reshape(TOP_LEVELS + 1, 4, RANK, RANK)
    eye = jnp.eye(RANK, dtype=jnp.float32)
    lift1 = up[0]
    lift2 = mm(lift1, up[1])
    lift3 = mm(lift2, up[2])
    lifts = jnp.stack([eye, lift1, lift2, lift3])
    push1 = down[0]
    push2 = mm(down[1], push1)
    push3 = mm(down[2], push2)
    pushes = jnp.stack([eye, push1, push2, push3])
    weights = jnp.einsum("sqkp,spm->sqkm", cross, pushes, precision=highest)

    p = jnp.einsum("rk,skq->srq", root_coefficients, lifts, precision=highest)

    bit0 = me & 1
    bit1 = (me >> 1) & 1
    bit2 = (me >> 2) & 1
    got1 = swap_with(p, 1)
    pairs0 = ordered(bit0, p[0:1], got1[0:1])
    coef1 = p[1] + got1[1]
    part2 = p[2] + got1[2]
    part3 = p[3] + got1[3]
    got2 = swap_with(jnp.concatenate([pairs0, coef1[None], part2[None], part3[None]]), 2)
    quads0 = ordered(bit1, pairs0, got2[0:2])
    pairs1 = ordered(bit1, coef1[None], got2[2:3])
    coef2 = part2 + got2[3]
    part3 = part3 + got2[4]
    got3 = swap_with(jnp.concatenate([quads0, pairs1, coef2[None], part3[None]]), 4)
    octs0 = ordered(bit2, quads0, got3[0:4])
    quads1 = ordered(bit2, pairs1, got3[4:6])
    pairs2 = ordered(bit2, coef2[None], got3[6:7])
    coef3 = (part3 + got3[7])[None]

    node = 8
    ahead1 = receive_from(jnp.concatenate([octs0[0:3], quads1[0:3], pairs2, coef3]), node)
    behind1 = receive_from(jnp.concatenate([octs0[5:8], quads1[1:4], pairs2, coef3]), -node)
    ahead2 = receive_from(jnp.concatenate([pairs2[0:1], coef3, ahead1[8:9]]), 2 * node)
    behind2 = receive_from(jnp.concatenate([pairs2[1:2], coef3, behind1[8:9]]), -2 * node)
    ahead3 = ahead2[2:3]
    behind3 = behind2[2:3]

    window0 = jnp.concatenate([behind1[0:3], octs0, ahead1[0:3]])
    window1 = jnp.concatenate([behind1[3:6], quads1, ahead1[3:6]])
    window2 = jnp.concatenate([behind2[0:1], behind1[6:8], pairs2, ahead1[6:8], ahead2[0:1]])
    steps = jnp.array(partner_steps, dtype=jnp.int32) + 3
    chosen0 = jnp.take(window0, (me & 7) + steps, axis=0, mode="clip")
    chosen1 = jnp.take(window1, ((me >> 1) & 3) + steps, axis=0, mode="clip")
    chosen2 = jnp.take(window2, bit2 + steps, axis=0, mode="clip")
    chosen3 = jnp.concatenate([behind3, behind2[1:2], ahead2[1:2], ahead3])
    chosen = jnp.stack([chosen0, chosen1, chosen2, chosen3])
    return jnp.einsum("sqrk,sqkm->rm", chosen, weights, precision=highest)


def local(
    sources,
    points,
    near_offsets,
    far_offsets,
    source_basis,
    target_basis,
    leaf_coupling,
    leaf_up,
    leaf_down,
    tree_up,
    tree_down,
    tree_coupling,
):
    leaf_count = near_offsets.shape[0]
    n = device_count()
    me = lax.axis_index("leaf") * lax.axis_size("grp") + lax.axis_index("grp")
    leaf_values = sources.reshape(RHS, leaf_count, CLUSTER)
    leaf_coefficients = jnp.einsum(
        "rla,lak->lrk",
        leaf_values,
        source_basis.reshape(leaf_count, CLUSTER, RANK),
        preferred_element_type=jnp.float32,
    )
    coef_rows = leaf_coefficients.reshape(leaf_count, RHS * RANK)

    packed = jnp.concatenate([sources.astype(jnp.float32), points], axis=0)
    width = NEAR_REACH * CLUSTER
    to_right = jnp.concatenate(
        [packed[:, -width:].reshape(-1), coef_rows[-FAR_REACH:].reshape(-1)]
    )
    to_left = jnp.concatenate([packed[:, :width].reshape(-1), coef_rows[:FAR_REACH].reshape(-1)])
    from_left = lax.ppermute(to_right, AXES, [(i, i + 1) for i in range(n - 1)])
    from_right = lax.ppermute(to_left, AXES, [(i + 1, i) for i in range(n - 1)])
    split = (RHS + 3) * width
    extended = jnp.concatenate(
        [
            from_left[:split].reshape(RHS + 3, width),
            packed,
            from_right[:split].reshape(RHS + 3, width),
        ],
        axis=1,
    ).reshape(RHS + 3, leaf_count + 2 * NEAR_REACH, CLUSTER)
    rimmed = jnp.concatenate(
        [
            from_left[split:].reshape(FAR_REACH, RHS * RANK),
            coef_rows,
            from_right[split:].reshape(FAR_REACH, RHS * RANK),
        ]
    )

    target_points = points.reshape(3, leaf_count, CLUSTER)
    near_sum = near_field(extended, target_points, near_offsets, leaf_values)

    far_index = jnp.arange(leaf_count, dtype=jnp.int32)[:, None] + FAR_REACH + far_offsets
    partner_blocks = jnp.take(rimmed, far_index, axis=0).reshape(leaf_count, FAR_BLOCKS, RHS, RANK)
    leaf_far = jnp.einsum(
        "lfrk,lfkq->lrq",
        partner_blocks,
        leaf_coupling.reshape(leaf_count, FAR_BLOCKS, RANK, RANK),
        precision=highest,
        preferred_element_type=jnp.float32,
    )
    root_coefficients = jnp.einsum(
        "lrk,lkq->rq",
        leaf_coefficients,
        leaf_up.reshape(leaf_count, RANK, RANK),
        precision=highest,
        preferred_element_type=jnp.float32,
    )
    downward = tree_field(root_coefficients, tree_up, tree_down, tree_coupling, me)
    from_root = jnp.einsum(
        "rk,lkq->lrq",
        downward,
        leaf_down.reshape(leaf_count, RANK, RANK),
        precision=highest,
        preferred_element_type=jnp.float32,
    )
    leaf_field = leaf_far + from_root
    far_out = jnp.einsum(
        "lrk,lka->rla",
        leaf_field,
        target_basis.reshape(leaf_count, RANK, CLUSTER),
        precision=highest,
        preferred_element_type=jnp.float32,
    )
    return (near_sum + far_out).reshape(RHS, leaf_count * CLUSTER)


def solution(mesh):
    placed = (
        P(None, AXES),
        P(None, AXES),
        P(AXES, None),
        P(AXES, None),
        P(AXES, None),
        P(AXES, None),
        P(AXES, None, None),
        P(AXES, None),
        P(AXES, None),
        P(AXES, None, None),
        P(AXES, None, None),
        P(AXES, None, None, None),
    )
    return jax.shard_map(
        local, mesh=mesh, in_specs=placed, out_specs=P(None, AXES), check_vma=False
    )
```

```python
import jax
import jax.numpy as jnp
from jax import lax
from jax.sharding import PartitionSpec as P

CLUSTER = 64
RANK = 32
RHS = 16
NEAR_REACH = 16
NEAR_BLOCKS = 6
FAR_REACH = 32
FAR_BLOCKS = 8
TOP_LEVELS = 3


amplitude = 0.15
length_scale = 1.0
nugget = 0.5
partner_steps = (-3, -2, 2, 3)
highest = lax.Precision.HIGHEST
AXES = ("leaf", "grp")


def device_count():
    return lax.axis_size("leaf") * lax.axis_size("grp")


def swap_with(value, mask):
    n = device_count()
    return lax.ppermute(value, AXES, [(i, i ^ mask) for i in range(n)])


def receive_from(value, step):
    n = device_count()
    return lax.ppermute(value, AXES, [(s, s - step) for s in range(n) if 0 <= s - step < n])


def near_field(extended, target_points, near_offsets, leaf_values):
    leaf_count = target_points.shape[1]
    column_count = extended.shape[0] - 3
    by_leaf = jnp.transpose(extended, (1, 0, 2))
    base = jnp.arange(leaf_count, dtype=jnp.int32) + NEAR_REACH
    chosen = jnp.concatenate(
        [
            jnp.take(by_leaf, base + near_offsets[:, near_slot], axis=0, mode="clip")
            for near_slot in range(NEAR_BLOCKS)
        ],
        axis=2,
    )
    chosen = jnp.transpose(chosen, (1, 0, 2))
    squared = jnp.zeros((leaf_count, CLUSTER, NEAR_BLOCKS * CLUSTER), jnp.float32)
    for component in range(3):
        separation = (
            chosen[column_count + component][:, None, :] - target_points[component][:, :, None]
        )
        squared = squared + separation * separation
    kernel = (amplitude * jnp.exp(-jnp.sqrt(squared) / length_scale)).astype(jnp.bfloat16)
    values = chosen[:column_count].astype(jnp.bfloat16)
    near = jnp.einsum("rlm,lbm->rlb", values, kernel, preferred_element_type=jnp.float32)
    return nugget * leaf_values.astype(jnp.float32) + near


def mm(a, b):
    return jnp.matmul(a, b, precision=highest, preferred_element_type=jnp.float32)


def ordered(bit, own, other):
    return jnp.where(bit == 0, jnp.concatenate([own, other]), jnp.concatenate([other, own]))


def tree_weights(tree_up, tree_down, tree_coupling):
    up = tree_up[0].astype(jnp.float32).reshape(TOP_LEVELS, RANK, RANK)
    down = tree_down[0].astype(jnp.float32).reshape(TOP_LEVELS, RANK, RANK)
    cross = tree_coupling[0].astype(jnp.float32).reshape(TOP_LEVELS + 1, 4, RANK, RANK)
    eye = jnp.eye(RANK, dtype=jnp.float32)
    lift1 = up[0]
    lift2 = mm(lift1, up[1])
    lift3 = mm(lift2, up[2])
    lifts = jnp.stack([eye, lift1, lift2, lift3])
    push1 = down[0]
    push2 = mm(down[1], push1)
    push3 = mm(down[2], push2)
    pushes = jnp.stack([eye, push1, push2, push3])
    weights = jnp.einsum("sqkp,spm->sqkm", cross, pushes, precision=highest)
    return lifts, weights


def tree_field(p, partner_p, weights, me):
    bit0 = me & 1
    pair = (me >> 1) & 3
    bit2 = (me >> 2) & 1
    pairs0 = ordered(bit0, p[0:1], partner_p[0:1])
    summed = p[1:4] + partner_p[1:4]
    mine = jnp.concatenate([pairs0, summed])
    held = jnp.stack([mine, swap_with(mine, 2), swap_with(mine, 4), swap_with(mine, 6)])
    node_pairs = jnp.take(held, pair ^ jnp.arange(4, dtype=jnp.int32), axis=0, mode="clip")
    octs0 = node_pairs[:, 0:2].reshape(8, RHS, RANK)
    quads1 = node_pairs[:, 2]
    pairs2 = node_pairs[0::2, 3] + node_pairs[1::2, 3]
    coef3 = jnp.sum(node_pairs[:, 4], axis=0)[None]

    node = 8
    ahead1 = receive_from(jnp.concatenate([octs0[0:3], quads1[0:3], pairs2, coef3]), node)
    behind1 = receive_from(jnp.concatenate([octs0[5:8], quads1[1:4], pairs2, coef3]), -node)
    ahead2 = receive_from(jnp.concatenate([pairs2[0:1], coef3, ahead1[8:9]]), 2 * node)
    behind2 = receive_from(jnp.concatenate([pairs2[1:2], coef3, behind1[8:9]]), -2 * node)
    ahead3 = ahead2[2:3]
    behind3 = behind2[2:3]

    window0 = jnp.concatenate([behind1[0:3], octs0, ahead1[0:3]])
    window1 = jnp.concatenate([behind1[3:6], quads1, ahead1[3:6]])
    window2 = jnp.concatenate([behind2[0:1], behind1[6:8], pairs2, ahead1[6:8], ahead2[0:1]])
    steps = jnp.array(partner_steps, dtype=jnp.int32) + 3
    chosen0 = jnp.take(window0, (me & 7) + steps, axis=0, mode="clip")
    chosen1 = jnp.take(window1, pair + steps, axis=0, mode="clip")
    chosen2 = jnp.take(window2, bit2 + steps, axis=0, mode="clip")
    chosen3 = jnp.concatenate([behind3, behind2[1:2], ahead2[1:2], ahead3])
    chosen = jnp.stack([chosen0, chosen1, chosen2, chosen3])
    return jnp.einsum("sqrk,sqkm->rm", chosen, weights, precision=highest)


def local(
    sources,
    points,
    near_offsets,
    far_offsets,
    source_basis,
    target_basis,
    leaf_coupling,
    leaf_up,
    leaf_down,
    tree_up,
    tree_down,
    tree_coupling,
):
    leaf_count = near_offsets.shape[0]
    n = device_count()
    me = lax.axis_index("leaf") * lax.axis_size("grp") + lax.axis_index("grp")
    leaf_values = sources.reshape(RHS, leaf_count, CLUSTER)
    leaf_coefficients = jnp.einsum(
        "rla,lak->lrk",
        leaf_values,
        source_basis.reshape(leaf_count, CLUSTER, RANK),
        preferred_element_type=jnp.float32,
    )
    coef_rows = leaf_coefficients.reshape(leaf_count, RHS * RANK)

    root_coefficients = jnp.einsum(
        "lrk,lkq->rq",
        leaf_coefficients,
        leaf_up.reshape(leaf_count, RANK, RANK),
        precision=highest,
        preferred_element_type=jnp.float32,
    )
    lifts, weights = tree_weights(tree_up, tree_down, tree_coupling)
    p = jnp.einsum("rk,skq->srq", root_coefficients, lifts, precision=highest)

    packed = jnp.concatenate([sources.astype(jnp.float32), points], axis=0)
    width = NEAR_REACH * CLUSTER
    to_right = jnp.concatenate(
        [packed[:, -width:].reshape(-1), coef_rows[-FAR_REACH:].reshape(-1), p.reshape(-1)]
    )
    to_left = jnp.concatenate(
        [packed[:, :width].reshape(-1), coef_rows[:FAR_REACH].reshape(-1), p.reshape(-1)]
    )
    from_left = lax.ppermute(to_right, AXES, [(i, i + 1) for i in range(n - 1)])
    from_right = lax.ppermute(to_left, AXES, [(i + 1, i) for i in range(n - 1)])
    split = (RHS + 3) * width
    split2 = split + FAR_REACH * RHS * RANK
    partner_p = jnp.where(
        (me & 1) == 0, from_right[split2:], from_left[split2:]
    ).reshape(TOP_LEVELS + 1, RHS, RANK)
    extended = jnp.concatenate(
        [
            from_left[:split].reshape(RHS + 3, width),
            packed,
            from_right[:split].reshape(RHS + 3, width),
        ],
        axis=1,
    ).reshape(RHS + 3, leaf_count + 2 * NEAR_REACH, CLUSTER)
    rimmed = jnp.concatenate(
        [
            from_left[split:split2].reshape(FAR_REACH, RHS * RANK),
            coef_rows,
            from_right[split:split2].reshape(FAR_REACH, RHS * RANK),
        ]
    )

    target_points = points.reshape(3, leaf_count, CLUSTER)
    near_sum = near_field(extended, target_points, near_offsets, leaf_values)

    far_index = jnp.arange(leaf_count, dtype=jnp.int32)[:, None] + FAR_REACH + far_offsets
    partner_blocks = jnp.take(rimmed, far_index, axis=0).reshape(leaf_count, FAR_BLOCKS, RHS, RANK)
    leaf_far = jnp.einsum(
        "lfrk,lfkq->lrq",
        partner_blocks,
        leaf_coupling.reshape(leaf_count, FAR_BLOCKS, RANK, RANK),
        precision=highest,
        preferred_element_type=jnp.float32,
    )
    downward = tree_field(p, partner_p, weights, me)
    from_root = jnp.einsum(
        "rk,lkq->lrq",
        downward,
        leaf_down.reshape(leaf_count, RANK, RANK),
        precision=highest,
        preferred_element_type=jnp.float32,
    )
    leaf_field = leaf_far + from_root
    far_out = jnp.einsum(
        "lrk,lka->rla",
        leaf_field,
        target_basis.reshape(leaf_count, RANK, CLUSTER),
        precision=highest,
        preferred_element_type=jnp.float32,
    )
    return (near_sum + far_out).reshape(RHS, leaf_count * CLUSTER)


def solution(mesh):
    placed = (
        P(None, AXES),
        P(None, AXES),
        P(AXES, None),
        P(AXES, None),
        P(AXES, None),
        P(AXES, None),
        P(AXES, None, None),
        P(AXES, None),
        P(AXES, None),
        P(AXES, None, None),
        P(AXES, None, None),
        P(AXES, None, None, None),
    )
    return jax.shard_map(
        local, mesh=mesh, in_specs=placed, out_specs=P(None, AXES), check_vma=False
    )
```

```python
import jax
import jax.numpy as jnp
from jax import lax
from jax.experimental import pallas as pl
from jax.experimental.pallas import tpu as pltpu
from jax.sharding import PartitionSpec as P

CLUSTER = 64
RANK = 32
RHS = 16
NEAR_REACH = 16
NEAR_BLOCKS = 6
FAR_REACH = 32
FAR_BLOCKS = 8
TOP_LEVELS = 3


amplitude = 0.15
length_scale = 1.0
nugget = 0.5
partner_steps = (-3, -2, 2, 3)
highest = lax.Precision.HIGHEST
AXES = ("leaf", "grp")


def device_count():
    return lax.axis_size("leaf") * lax.axis_size("grp")


def swap_with(value, mask):
    n = device_count()
    return lax.ppermute(value, AXES, [(i, i ^ mask) for i in range(n)])


def receive_from(value, step):
    n = device_count()
    return lax.ppermute(value, AXES, [(s, s - step) for s in range(n) if 0 <= s - step < n])


def near_body(offsets_ref, table_ref, columns_ref, out_ref):
    leaf_count = out_ref.shape[0]
    rows = RHS + 3
    lane = lax.broadcasted_iota(jnp.int32, (rows, 2 * CLUSTER), 1)
    low_half = lane < CLUSTER

    def one_leaf(i, carry):
        own = table_ref[i + NEAR_REACH]
        total = nugget * own[:RHS, :CLUSTER]
        columns = columns_ref[i]
        for pair in range(NEAR_BLOCKS // 2):
            first = table_ref[i + NEAR_REACH + offsets_ref[i, 2 * pair]]
            second = table_ref[i + NEAR_REACH + offsets_ref[i, 2 * pair + 1]]
            joined = jnp.where(low_half, first, second)
            squared = None
            for component in range(3):
                separation = joined[RHS + component : RHS + component + 1, :] - columns[:, component : component + 1]
                term = separation * separation
                squared = term if squared is None else squared + term
            kernel = (amplitude * jnp.exp(-jnp.sqrt(squared) / length_scale)).astype(jnp.bfloat16)
            values = joined[:RHS].astype(jnp.bfloat16)
            total = total + lax.dot_general(
                values, kernel, (((1,), (1,)), ((), ())), preferred_element_type=jnp.float32
            )
        out_ref[i] = total
        return carry

    lax.fori_loop(0, leaf_count, one_leaf, 0)


def near_field_kernel(extended, target_points, near_offsets):
    leaf_count = target_points.shape[1]
    by_leaf = jnp.transpose(extended, (1, 0, 2))
    table = jnp.concatenate([by_leaf, by_leaf], axis=2)
    columns = jnp.pad(jnp.transpose(target_points, (1, 2, 0)), ((0, 0), (0, 0), (0, 125)))
    return pl.pallas_call(
        near_body,
        out_shape=jax.ShapeDtypeStruct((leaf_count, RHS, CLUSTER), jnp.float32),
        in_specs=[
            pl.BlockSpec(memory_space=pltpu.SMEM),
            pl.BlockSpec(memory_space=pltpu.VMEM),
            pl.BlockSpec(memory_space=pltpu.VMEM),
        ],
        out_specs=pl.BlockSpec(memory_space=pltpu.VMEM),
    )(near_offsets, table, columns)


def mm(a, b):
    return jnp.matmul(a, b, precision=highest, preferred_element_type=jnp.float32)


def ordered(bit, own, other):
    return jnp.where(bit == 0, jnp.concatenate([own, other]), jnp.concatenate([other, own]))


def tree_field(root_coefficients, tree_up, tree_down, tree_coupling, me):
    up = tree_up[0].astype(jnp.float32).reshape(TOP_LEVELS, RANK, RANK)
    down = tree_down[0].astype(jnp.float32).reshape(TOP_LEVELS, RANK, RANK)
    cross = tree_coupling[0].astype(jnp.float32).reshape(TOP_LEVELS + 1, 4, RANK, RANK)
    eye = jnp.eye(RANK, dtype=jnp.float32)
    lift1 = up[0]
    lift2 = mm(lift1, up[1])
    lift3 = mm(lift2, up[2])
    lifts = jnp.stack([eye, lift1, lift2, lift3])
    push1 = down[0]
    push2 = mm(down[1], push1)
    push3 = mm(down[2], push2)
    pushes = jnp.stack([eye, push1, push2, push3])
    weights = jnp.einsum("sqkp,spm->sqkm", cross, pushes, precision=highest)

    p = jnp.einsum("rk,skq->srq", root_coefficients, lifts, precision=highest)

    bit0 = me & 1
    bit1 = (me >> 1) & 1
    bit2 = (me >> 2) & 1
    got1 = swap_with(p, 1)
    pairs0 = ordered(bit0, p[0:1], got1[0:1])
    coef1 = p[1] + got1[1]
    part2 = p[2] + got1[2]
    part3 = p[3] + got1[3]
    got2 = swap_with(jnp.concatenate([pairs0, coef1[None], part2[None], part3[None]]), 2)
    quads0 = ordered(bit1, pairs0, got2[0:2])
    pairs1 = ordered(bit1, coef1[None], got2[2:3])
    coef2 = part2 + got2[3]
    part3 = part3 + got2[4]
    got3 = swap_with(jnp.concatenate([quads0, pairs1, coef2[None], part3[None]]), 4)
    octs0 = ordered(bit2, quads0, got3[0:4])
    quads1 = ordered(bit2, pairs1, got3[4:6])
    pairs2 = ordered(bit2, coef2[None], got3[6:7])
    coef3 = (part3 + got3[7])[None]

    node = 8
    ahead1 = receive_from(jnp.concatenate([octs0[0:3], quads1[0:3], pairs2, coef3]), node)
    behind1 = receive_from(jnp.concatenate([octs0[5:8], quads1[1:4], pairs2, coef3]), -node)
    ahead2 = receive_from(jnp.concatenate([pairs2[0:1], coef3, ahead1[8:9]]), 2 * node)
    behind2 = receive_from(jnp.concatenate([pairs2[1:2], coef3, behind1[8:9]]), -2 * node)
    ahead3 = ahead2[2:3]
    behind3 = behind2[2:3]

    window0 = jnp.concatenate([behind1[0:3], octs0, ahead1[0:3]])
    window1 = jnp.concatenate([behind1[3:6], quads1, ahead1[3:6]])
    window2 = jnp.concatenate([behind2[0:1], behind1[6:8], pairs2, ahead1[6:8], ahead2[0:1]])
    steps = jnp.array(partner_steps, dtype=jnp.int32) + 3
    chosen0 = jnp.take(window0, (me & 7) + steps, axis=0, mode="clip")
    chosen1 = jnp.take(window1, ((me >> 1) & 3) + steps, axis=0, mode="clip")
    chosen2 = jnp.take(window2, bit2 + steps, axis=0, mode="clip")
    chosen3 = jnp.concatenate([behind3, behind2[1:2], ahead2[1:2], ahead3])
    chosen = jnp.stack([chosen0, chosen1, chosen2, chosen3])
    return jnp.einsum("sqrk,sqkm->rm", chosen, weights, precision=highest)


def local(
    sources,
    points,
    near_offsets,
    far_offsets,
    source_basis,
    target_basis,
    leaf_coupling,
    leaf_up,
    leaf_down,
    tree_up,
    tree_down,
    tree_coupling,
):
    leaf_count = near_offsets.shape[0]
    n = device_count()
    me = lax.axis_index("leaf") * lax.axis_size("grp") + lax.axis_index("grp")
    leaf_values = sources.reshape(RHS, leaf_count, CLUSTER)
    leaf_coefficients = jnp.einsum(
        "rla,lak->lrk",
        leaf_values,
        source_basis.reshape(leaf_count, CLUSTER, RANK),
        preferred_element_type=jnp.float32,
    )
    coef_rows = leaf_coefficients.reshape(leaf_count, RHS * RANK)

    packed = jnp.concatenate([sources.astype(jnp.float32), points], axis=0)
    width = NEAR_REACH * CLUSTER
    to_right = jnp.concatenate(
        [packed[:, -width:].reshape(-1), coef_rows[-FAR_REACH:].reshape(-1)]
    )
    to_left = jnp.concatenate([packed[:, :width].reshape(-1), coef_rows[:FAR_REACH].reshape(-1)])
    from_left = lax.ppermute(to_right, AXES, [(i, i + 1) for i in range(n - 1)])
    from_right = lax.ppermute(to_left, AXES, [(i + 1, i) for i in range(n - 1)])
    split = (RHS + 3) * width
    extended = jnp.concatenate(
        [
            from_left[:split].reshape(RHS + 3, width),
            packed,
            from_right[:split].reshape(RHS + 3, width),
        ],
        axis=1,
    ).reshape(RHS + 3, leaf_count + 2 * NEAR_REACH, CLUSTER)
    rimmed = jnp.concatenate(
        [
            from_left[split:].reshape(FAR_REACH, RHS * RANK),
            coef_rows,
            from_right[split:].reshape(FAR_REACH, RHS * RANK),
        ]
    )

    target_points = points.reshape(3, leaf_count, CLUSTER)
    near_sum = near_field_kernel(extended, target_points, near_offsets)

    far_index = jnp.arange(leaf_count, dtype=jnp.int32)[:, None] + FAR_REACH + far_offsets
    partner_blocks = jnp.take(rimmed, far_index, axis=0).reshape(leaf_count, FAR_BLOCKS, RHS, RANK)
    leaf_far = jnp.einsum(
        "lfrk,lfkq->lrq",
        partner_blocks,
        leaf_coupling.reshape(leaf_count, FAR_BLOCKS, RANK, RANK),
        precision=highest,
        preferred_element_type=jnp.float32,
    )
    root_coefficients = jnp.einsum(
        "lrk,lkq->rq",
        leaf_coefficients,
        leaf_up.reshape(leaf_count, RANK, RANK),
        precision=highest,
        preferred_element_type=jnp.float32,
    )
    downward = tree_field(root_coefficients, tree_up, tree_down, tree_coupling, me)
    from_root = jnp.einsum(
        "rk,lkq->lrq",
        downward,
        leaf_down.reshape(leaf_count, RANK, RANK),
        precision=highest,
        preferred_element_type=jnp.float32,
    )
    leaf_field = leaf_far + from_root
    far_out = jnp.einsum(
        "lrk,lka->lra",
        leaf_field,
        target_basis.reshape(leaf_count, RANK, CLUSTER),
        precision=highest,
        preferred_element_type=jnp.float32,
    )
    product = jnp.transpose(near_sum + far_out, (1, 0, 2))
    return product.reshape(RHS, leaf_count * CLUSTER)


def solution(mesh):
    placed = (
        P(None, AXES),
        P(None, AXES),
        P(AXES, None),
        P(AXES, None),
        P(AXES, None),
        P(AXES, None),
        P(AXES, None, None),
        P(AXES, None),
        P(AXES, None),
        P(AXES, None, None),
        P(AXES, None, None),
        P(AXES, None, None, None),
    )
    return jax.shard_map(
        local, mesh=mesh, in_specs=placed, out_specs=P(None, AXES), check_vma=False
    )
```

```python
import jax
import jax.numpy as jnp
from jax import lax
from jax.experimental import pallas as pl
from jax.experimental.pallas import tpu as pltpu
from jax.sharding import PartitionSpec as P

CLUSTER = 64
RANK = 32
RHS = 16
NEAR_REACH = 16
NEAR_BLOCKS = 6
FAR_REACH = 32
FAR_BLOCKS = 8
TOP_LEVELS = 3


amplitude = 0.15
length_scale = 1.0
nugget = 0.5
partner_steps = (-3, -2, 2, 3)
highest = lax.Precision.HIGHEST
AXES = ("leaf", "grp")


def device_count():
    return lax.axis_size("leaf") * lax.axis_size("grp")


def swap_with(value, mask):
    n = device_count()
    return lax.ppermute(value, AXES, [(i, i ^ mask) for i in range(n)])


def receive_from(value, step):
    n = device_count()
    return lax.ppermute(value, AXES, [(s, s - step) for s in range(n) if 0 <= s - step < n])


def near_body(offsets_ref, table_ref, columns_ref, out_ref):
    leaf_count = out_ref.shape[0]
    rows = RHS + 3
    lane = lax.broadcasted_iota(jnp.int32, (rows, 2 * CLUSTER), 1)
    low_half = lane < CLUSTER

    def one_leaf(i, carry):
        own = table_ref[i + NEAR_REACH]
        parts = []
        columns = columns_ref[i]
        for pair in range(NEAR_BLOCKS // 2):
            first = table_ref[i + NEAR_REACH + offsets_ref[i, 2 * pair]]
            second = table_ref[i + NEAR_REACH + offsets_ref[i, 2 * pair + 1]]
            joined = jnp.where(low_half, first, second)
            squared = None
            for component in range(3):
                separation = joined[RHS + component : RHS + component + 1, :] - columns[:, component : component + 1]
                term = separation * separation
                squared = term if squared is None else squared + term
            kernel = (amplitude * jnp.exp(-jnp.sqrt(squared) / length_scale)).astype(jnp.bfloat16)
            values = joined[:RHS].astype(jnp.bfloat16)
            parts.append(
                lax.dot_general(
                    values, kernel, (((1,), (1,)), ((), ())), preferred_element_type=jnp.float32
                )
            )
        out_ref[i] = nugget * own[:RHS, :CLUSTER] + (parts[0] + parts[1] + parts[2])
        return carry

    lax.fori_loop(0, leaf_count, one_leaf, 0, unroll=8)


def near_field_kernel(extended, target_points, near_offsets):
    leaf_count = target_points.shape[1]
    by_leaf = jnp.transpose(extended, (1, 0, 2))
    table = jnp.concatenate([by_leaf, by_leaf], axis=2)
    columns = jnp.pad(jnp.transpose(target_points, (1, 2, 0)), ((0, 0), (0, 0), (0, 125)))
    return pl.pallas_call(
        near_body,
        out_shape=jax.ShapeDtypeStruct((leaf_count, RHS, CLUSTER), jnp.float32),
        in_specs=[
            pl.BlockSpec(memory_space=pltpu.SMEM),
            pl.BlockSpec(memory_space=pltpu.VMEM),
            pl.BlockSpec(memory_space=pltpu.VMEM),
        ],
        out_specs=pl.BlockSpec(memory_space=pltpu.VMEM),
    )(near_offsets, table, columns)


def mm(a, b):
    return jnp.matmul(a, b, precision=highest, preferred_element_type=jnp.float32)


def ordered(bit, own, other):
    return jnp.where(bit == 0, jnp.concatenate([own, other]), jnp.concatenate([other, own]))


def tree_field(root_coefficients, tree_up, tree_down, tree_coupling, me):
    up = tree_up[0].astype(jnp.float32).reshape(TOP_LEVELS, RANK, RANK)
    down = tree_down[0].astype(jnp.float32).reshape(TOP_LEVELS, RANK, RANK)
    cross = tree_coupling[0].astype(jnp.float32).reshape(TOP_LEVELS + 1, 4, RANK, RANK)
    eye = jnp.eye(RANK, dtype=jnp.float32)
    lift1 = up[0]
    lift2 = mm(lift1, up[1])
    lift3 = mm(lift2, up[2])
    lifts = jnp.stack([eye, lift1, lift2, lift3])
    push1 = down[0]
    push2 = mm(down[1], push1)
    push3 = mm(down[2], push2)
    pushes = jnp.stack([eye, push1, push2, push3])
    weights = jnp.einsum("sqkp,spm->sqkm", cross, pushes, precision=highest)

    p = jnp.einsum("rk,skq->srq", root_coefficients, lifts, precision=highest)

    bit0 = me & 1
    bit1 = (me >> 1) & 1
    bit2 = (me >> 2) & 1
    got1 = swap_with(p, 1)
    pairs0 = ordered(bit0, p[0:1], got1[0:1])
    coef1 = p[1] + got1[1]
    part2 = p[2] + got1[2]
    part3 = p[3] + got1[3]
    got2 = swap_with(jnp.concatenate([pairs0, coef1[None], part2[None], part3[None]]), 2)
    quads0 = ordered(bit1, pairs0, got2[0:2])
    pairs1 = ordered(bit1, coef1[None], got2[2:3])
    coef2 = part2 + got2[3]
    part3 = part3 + got2[4]
    got3 = swap_with(jnp.concatenate([quads0, pairs1, coef2[None], part3[None]]), 4)
    octs0 = ordered(bit2, quads0, got3[0:4])
    quads1 = ordered(bit2, pairs1, got3[4:6])
    pairs2 = ordered(bit2, coef2[None], got3[6:7])
    coef3 = (part3 + got3[7])[None]

    node = 8
    ahead1 = receive_from(jnp.concatenate([octs0[0:3], quads1[0:3], pairs2, coef3]), node)
    behind1 = receive_from(jnp.concatenate([octs0[5:8], quads1[1:4], pairs2, coef3]), -node)
    ahead2 = receive_from(jnp.concatenate([pairs2[0:1], coef3, ahead1[8:9]]), 2 * node)
    behind2 = receive_from(jnp.concatenate([pairs2[1:2], coef3, behind1[8:9]]), -2 * node)
    ahead3 = ahead2[2:3]
    behind3 = behind2[2:3]

    window0 = jnp.concatenate([behind1[0:3], octs0, ahead1[0:3]])
    window1 = jnp.concatenate([behind1[3:6], quads1, ahead1[3:6]])
    window2 = jnp.concatenate([behind2[0:1], behind1[6:8], pairs2, ahead1[6:8], ahead2[0:1]])
    steps = jnp.array(partner_steps, dtype=jnp.int32) + 3
    chosen0 = jnp.take(window0, (me & 7) + steps, axis=0, mode="clip")
    chosen1 = jnp.take(window1, ((me >> 1) & 3) + steps, axis=0, mode="clip")
    chosen2 = jnp.take(window2, bit2 + steps, axis=0, mode="clip")
    chosen3 = jnp.concatenate([behind3, behind2[1:2], ahead2[1:2], ahead3])
    chosen = jnp.stack([chosen0, chosen1, chosen2, chosen3])
    return jnp.einsum("sqrk,sqkm->rm", chosen, weights, precision=highest)


def local(
    sources,
    points,
    near_offsets,
    far_offsets,
    source_basis,
    target_basis,
    leaf_coupling,
    leaf_up,
    leaf_down,
    tree_up,
    tree_down,
    tree_coupling,
):
    leaf_count = near_offsets.shape[0]
    n = device_count()
    me = lax.axis_index("leaf") * lax.axis_size("grp") + lax.axis_index("grp")
    leaf_values = sources.reshape(RHS, leaf_count, CLUSTER)
    leaf_coefficients = jnp.einsum(
        "rla,lak->lrk",
        leaf_values,
        source_basis.reshape(leaf_count, CLUSTER, RANK),
        preferred_element_type=jnp.float32,
    )
    coef_rows = leaf_coefficients.reshape(leaf_count, RHS * RANK)

    packed = jnp.concatenate([sources.astype(jnp.float32), points], axis=0)
    width = NEAR_REACH * CLUSTER
    to_right = jnp.concatenate(
        [packed[:, -width:].reshape(-1), coef_rows[-FAR_REACH:].reshape(-1)]
    )
    to_left = jnp.concatenate([packed[:, :width].reshape(-1), coef_rows[:FAR_REACH].reshape(-1)])
    from_left = lax.ppermute(to_right, AXES, [(i, i + 1) for i in range(n - 1)])
    from_right = lax.ppermute(to_left, AXES, [(i + 1, i) for i in range(n - 1)])
    split = (RHS + 3) * width
    extended = jnp.concatenate(
        [
            from_left[:split].reshape(RHS + 3, width),
            packed,
            from_right[:split].reshape(RHS + 3, width),
        ],
        axis=1,
    ).reshape(RHS + 3, leaf_count + 2 * NEAR_REACH, CLUSTER)
    rimmed = jnp.concatenate(
        [
            from_left[split:].reshape(FAR_REACH, RHS * RANK),
            coef_rows,
            from_right[split:].reshape(FAR_REACH, RHS * RANK),
        ]
    )

    target_points = points.reshape(3, leaf_count, CLUSTER)
    near_sum = near_field_kernel(extended, target_points, near_offsets)

    far_index = jnp.arange(leaf_count, dtype=jnp.int32)[:, None] + FAR_REACH + far_offsets
    partner_blocks = jnp.take(rimmed, far_index, axis=0).reshape(leaf_count, FAR_BLOCKS, RHS, RANK)
    leaf_far = jnp.einsum(
        "lfrk,lfkq->lrq",
        partner_blocks,
        leaf_coupling.reshape(leaf_count, FAR_BLOCKS, RANK, RANK),
        precision=highest,
        preferred_element_type=jnp.float32,
    )
    root_coefficients = jnp.einsum(
        "lrk,lkq->rq",
        leaf_coefficients,
        leaf_up.reshape(leaf_count, RANK, RANK),
        precision=highest,
        preferred_element_type=jnp.float32,
    )
    downward = tree_field(root_coefficients, tree_up, tree_down, tree_coupling, me)
    from_root = jnp.einsum(
        "rk,lkq->lrq",
        downward,
        leaf_down.reshape(leaf_count, RANK, RANK),
        precision=highest,
        preferred_element_type=jnp.float32,
    )
    leaf_field = leaf_far + from_root
    far_out = jnp.einsum(
        "lrk,lka->lra",
        leaf_field,
        target_basis.reshape(leaf_count, RANK, CLUSTER),
        precision=highest,
        preferred_element_type=jnp.float32,
    )
    product = jnp.transpose(near_sum + far_out, (1, 0, 2))
    return product.reshape(RHS, leaf_count * CLUSTER)


def solution(mesh):
    placed = (
        P(None, AXES),
        P(None, AXES),
        P(AXES, None),
        P(AXES, None),
        P(AXES, None),
        P(AXES, None),
        P(AXES, None, None),
        P(AXES, None),
        P(AXES, None),
        P(AXES, None, None),
        P(AXES, None, None),
        P(AXES, None, None, None),
    )
    return jax.shard_map(
        local, mesh=mesh, in_specs=placed, out_specs=P(None, AXES), check_vma=False
    )
```

```python
import jax
import jax.numpy as jnp
from jax import lax
from jax.experimental import pallas as pl
from jax.experimental.pallas import tpu as pltpu
from jax.sharding import PartitionSpec as P

CLUSTER = 64
RANK = 32
RHS = 16
NEAR_REACH = 16
NEAR_BLOCKS = 6
FAR_REACH = 32
FAR_BLOCKS = 8
TOP_LEVELS = 3


amplitude = 0.15
length_scale = 1.0
nugget = 0.5
partner_steps = (-3, -2, 2, 3)
highest = lax.Precision.HIGHEST
bf16_weights = lax.Precision.HIGH
AXES = ("leaf", "grp")


def device_count():
    return lax.axis_size("leaf") * lax.axis_size("grp")


def swap_with(value, mask):
    n = device_count()
    return lax.ppermute(value, AXES, [(i, i ^ mask) for i in range(n)])


def receive_from(value, step):
    n = device_count()
    return lax.ppermute(value, AXES, [(s, s - step) for s in range(n) if 0 <= s - step < n])


def near_body(offsets_ref, table_ref, columns_ref, out_ref):
    leaf_count = out_ref.shape[0]
    rows = RHS + 3
    lane = lax.broadcasted_iota(jnp.int32, (rows, 2 * CLUSTER), 1)
    low_half = lane < CLUSTER

    def one_leaf(i, carry):
        own = table_ref[i + NEAR_REACH]
        parts = []
        columns = columns_ref[i]
        for pair in range(NEAR_BLOCKS // 2):
            first = table_ref[i + NEAR_REACH + offsets_ref[i, 2 * pair]]
            second = table_ref[i + NEAR_REACH + offsets_ref[i, 2 * pair + 1]]
            joined = jnp.where(low_half, first, second)
            squared = None
            for component in range(3):
                separation = joined[RHS + component : RHS + component + 1, :] - columns[:, component : component + 1]
                term = separation * separation
                squared = term if squared is None else squared + term
            kernel = (amplitude * jnp.exp(-jnp.sqrt(squared) / length_scale)).astype(jnp.bfloat16)
            values = joined[:RHS].astype(jnp.bfloat16)
            parts.append(
                lax.dot_general(
                    values, kernel, (((1,), (1,)), ((), ())), preferred_element_type=jnp.float32
                )
            )
        out_ref[i] = nugget * own[:RHS, :CLUSTER] + (parts[0] + parts[1] + parts[2])
        return carry

    lax.fori_loop(0, leaf_count, one_leaf, 0, unroll=16)


def near_field_kernel(extended, target_points, near_offsets):
    leaf_count = target_points.shape[1]
    by_leaf = jnp.transpose(extended, (1, 0, 2))
    table = jnp.concatenate([by_leaf, by_leaf], axis=2)
    columns = jnp.pad(jnp.transpose(target_points, (1, 2, 0)), ((0, 0), (0, 0), (0, 125)))
    return pl.pallas_call(
        near_body,
        out_shape=jax.ShapeDtypeStruct((leaf_count, RHS, CLUSTER), jnp.float32),
        in_specs=[
            pl.BlockSpec(memory_space=pltpu.SMEM),
            pl.BlockSpec(memory_space=pltpu.VMEM),
            pl.BlockSpec(memory_space=pltpu.VMEM),
        ],
        out_specs=pl.BlockSpec(memory_space=pltpu.VMEM),
    )(near_offsets, table, columns)


def mm(a, b):
    return jnp.matmul(a, b, precision=highest, preferred_element_type=jnp.float32)


def ordered(bit, own, other):
    return jnp.where(bit == 0, jnp.concatenate([own, other]), jnp.concatenate([other, own]))


def tree_field(root_coefficients, tree_up, tree_down, tree_coupling, me):
    up = tree_up[0].astype(jnp.float32).reshape(TOP_LEVELS, RANK, RANK)
    down = tree_down[0].astype(jnp.float32).reshape(TOP_LEVELS, RANK, RANK)
    cross = tree_coupling[0].astype(jnp.float32).reshape(TOP_LEVELS + 1, 4, RANK, RANK)
    eye = jnp.eye(RANK, dtype=jnp.float32)
    lift1 = up[0]
    lift2 = mm(lift1, up[1])
    lift3 = mm(lift2, up[2])
    lifts = jnp.stack([eye, lift1, lift2, lift3])
    push1 = down[0]
    push2 = mm(down[1], push1)
    push3 = mm(down[2], push2)
    pushes = jnp.stack([eye, push1, push2, push3])
    weights = jnp.einsum("sqkp,spm->sqkm", cross, pushes, precision=highest)

    p = jnp.einsum("rk,skq->srq", root_coefficients, lifts, precision=highest)

    bit0 = me & 1
    bit1 = (me >> 1) & 1
    bit2 = (me >> 2) & 1
    got1 = swap_with(p, 1)
    pairs0 = ordered(bit0, p[0:1], got1[0:1])
    coef1 = p[1] + got1[1]
    part2 = p[2] + got1[2]
    part3 = p[3] + got1[3]
    got2 = swap_with(jnp.concatenate([pairs0, coef1[None], part2[None], part3[None]]), 2)
    quads0 = ordered(bit1, pairs0, got2[0:2])
    pairs1 = ordered(bit1, coef1[None], got2[2:3])
    coef2 = part2 + got2[3]
    part3 = part3 + got2[4]
    got3 = swap_with(jnp.concatenate([quads0, pairs1, coef2[None], part3[None]]), 4)
    octs0 = ordered(bit2, quads0, got3[0:4])
    quads1 = ordered(bit2, pairs1, got3[4:6])
    pairs2 = ordered(bit2, coef2[None], got3[6:7])
    coef3 = (part3 + got3[7])[None]

    node = 8
    ahead1 = receive_from(jnp.concatenate([octs0[0:3], quads1[0:3], pairs2, coef3]), node)
    behind1 = receive_from(jnp.concatenate([octs0[5:8], quads1[1:4], pairs2, coef3]), -node)
    ahead2 = receive_from(jnp.concatenate([pairs2[0:1], coef3, ahead1[8:9]]), 2 * node)
    behind2 = receive_from(jnp.concatenate([pairs2[1:2], coef3, behind1[8:9]]), -2 * node)
    ahead3 = ahead2[2:3]
    behind3 = behind2[2:3]

    window0 = jnp.concatenate([behind1[0:3], octs0, ahead1[0:3]])
    window1 = jnp.concatenate([behind1[3:6], quads1, ahead1[3:6]])
    window2 = jnp.concatenate([behind2[0:1], behind1[6:8], pairs2, ahead1[6:8], ahead2[0:1]])
    steps = jnp.array(partner_steps, dtype=jnp.int32) + 3
    chosen0 = jnp.take(window0, (me & 7) + steps, axis=0, mode="clip")
    chosen1 = jnp.take(window1, ((me >> 1) & 3) + steps, axis=0, mode="clip")
    chosen2 = jnp.take(window2, bit2 + steps, axis=0, mode="clip")
    chosen3 = jnp.concatenate([behind3, behind2[1:2], ahead2[1:2], ahead3])
    chosen = jnp.stack([chosen0, chosen1, chosen2, chosen3])
    return jnp.einsum("sqrk,sqkm->rm", chosen, weights, precision=highest)


def local(
    sources,
    points,
    near_offsets,
    far_offsets,
    source_basis,
    target_basis,
    leaf_coupling,
    leaf_up,
    leaf_down,
    tree_up,
    tree_down,
    tree_coupling,
):
    leaf_count = near_offsets.shape[0]
    n = device_count()
    me = lax.axis_index("leaf") * lax.axis_size("grp") + lax.axis_index("grp")
    leaf_values = sources.reshape(RHS, leaf_count, CLUSTER)
    leaf_coefficients = jnp.einsum(
        "rla,lak->lrk",
        leaf_values,
        source_basis.reshape(leaf_count, CLUSTER, RANK),
        preferred_element_type=jnp.float32,
    )
    coef_rows = leaf_coefficients.reshape(leaf_count, RHS * RANK)

    packed = jnp.concatenate([sources.astype(jnp.float32), points], axis=0)
    width = NEAR_REACH * CLUSTER
    to_right = jnp.concatenate(
        [packed[:, -width:].reshape(-1), coef_rows[-FAR_REACH:].reshape(-1)]
    )
    to_left = jnp.concatenate([packed[:, :width].reshape(-1), coef_rows[:FAR_REACH].reshape(-1)])
    from_left = lax.ppermute(to_right, AXES, [(i, i + 1) for i in range(n - 1)])
    from_right = lax.ppermute(to_left, AXES, [(i + 1, i) for i in range(n - 1)])
    split = (RHS + 3) * width
    extended = jnp.concatenate(
        [
            from_left[:split].reshape(RHS + 3, width),
            packed,
            from_right[:split].reshape(RHS + 3, width),
        ],
        axis=1,
    ).reshape(RHS + 3, leaf_count + 2 * NEAR_REACH, CLUSTER)
    rimmed = jnp.concatenate(
        [
            from_left[split:].reshape(FAR_REACH, RHS * RANK),
            coef_rows,
            from_right[split:].reshape(FAR_REACH, RHS * RANK),
        ]
    )

    target_points = points.reshape(3, leaf_count, CLUSTER)
    near_sum = near_field_kernel(extended, target_points, near_offsets)

    far_index = jnp.arange(leaf_count, dtype=jnp.int32)[:, None] + FAR_REACH + far_offsets
    partner_blocks = jnp.take(rimmed, far_index, axis=0).reshape(leaf_count, FAR_BLOCKS, RHS, RANK)
    leaf_far = jnp.einsum(
        "lfrk,lfkq->lrq",
        partner_blocks,
        leaf_coupling.reshape(leaf_count, FAR_BLOCKS, RANK, RANK),
        precision=bf16_weights,
        preferred_element_type=jnp.float32,
    )
    root_coefficients = jnp.einsum(
        "lrk,lkq->rq",
        leaf_coefficients,
        leaf_up.reshape(leaf_count, RANK, RANK),
        precision=bf16_weights,
        preferred_element_type=jnp.float32,
    )
    downward = tree_field(root_coefficients, tree_up, tree_down, tree_coupling, me)
    from_root = jnp.einsum(
        "rk,lkq->lrq",
        downward,
        leaf_down.reshape(leaf_count, RANK, RANK),
        precision=bf16_weights,
        preferred_element_type=jnp.float32,
    )
    leaf_field = leaf_far + from_root
    far_out = jnp.einsum(
        "lrk,lka->lra",
        leaf_field,
        target_basis.reshape(leaf_count, RANK, CLUSTER),
        precision=bf16_weights,
        preferred_element_type=jnp.float32,
    )
    product = jnp.transpose(near_sum + far_out, (1, 0, 2))
    return product.reshape(RHS, leaf_count * CLUSTER)


def solution(mesh):
    placed = (
        P(None, AXES),
        P(None, AXES),
        P(AXES, None),
        P(AXES, None),
        P(AXES, None),
        P(AXES, None),
        P(AXES, None, None),
        P(AXES, None),
        P(AXES, None),
        P(AXES, None, None),
        P(AXES, None, None),
        P(AXES, None, None, None),
    )
    return jax.shard_map(
        local, mesh=mesh, in_specs=placed, out_specs=P(None, AXES), check_vma=False
    )
```

```python
import jax
import jax.numpy as jnp
from jax import lax
from jax.experimental import pallas as pl
from jax.experimental.pallas import tpu as pltpu
from jax.sharding import PartitionSpec as P

CLUSTER = 64
RANK = 32
RHS = 16
NEAR_REACH = 16
NEAR_BLOCKS = 6
FAR_REACH = 32
FAR_BLOCKS = 8
TOP_LEVELS = 3


amplitude = 0.15
length_scale = 1.0
nugget = 0.5
partner_steps = (-3, -2, 2, 3)
highest = lax.Precision.HIGHEST
bf16_weights = lax.Precision.HIGH
AXES = ("leaf", "grp")


def device_count():
    return lax.axis_size("leaf") * lax.axis_size("grp")


def swap_with(value, mask):
    n = device_count()
    return lax.ppermute(value, AXES, [(i, i ^ mask) for i in range(n)])


def receive_from(value, step):
    n = device_count()
    return lax.ppermute(value, AXES, [(s, s - step) for s in range(n) if 0 <= s - step < n])


def near_body(offsets_ref, table_ref, columns_ref, out_ref):
    leaf_count = out_ref.shape[0]
    rows = RHS + 3
    lane = lax.broadcasted_iota(jnp.int32, (rows, 2 * CLUSTER), 1)
    low_half = lane < CLUSTER

    def one_leaf(i, carry):
        own = table_ref[i + NEAR_REACH]
        parts = []
        columns = columns_ref[i]
        for pair in range(NEAR_BLOCKS // 2):
            first = table_ref[i + NEAR_REACH + offsets_ref[i, 2 * pair]]
            second = table_ref[i + NEAR_REACH + offsets_ref[i, 2 * pair + 1]]
            joined = jnp.where(low_half, first, second)
            squared = None
            for component in range(3):
                separation = joined[RHS + component : RHS + component + 1, :] - columns[:, component : component + 1]
                term = separation * separation
                squared = term if squared is None else squared + term
            kernel = (amplitude * jnp.exp(-jnp.sqrt(squared) / length_scale)).astype(jnp.bfloat16)
            values = joined[:RHS].astype(jnp.bfloat16)
            parts.append(
                lax.dot_general(
                    values, kernel, (((1,), (1,)), ((), ())), preferred_element_type=jnp.float32
                )
            )
        out_ref[i] = nugget * own[:RHS, :CLUSTER] + (parts[0] + parts[1] + parts[2])
        return carry

    lax.fori_loop(0, leaf_count, one_leaf, 0, unroll=16)


def near_field_kernel(extended, target_points, near_offsets):
    leaf_count = target_points.shape[1]
    by_leaf = jnp.transpose(extended, (1, 0, 2))
    table = jnp.concatenate([by_leaf, by_leaf], axis=2)
    columns = jnp.pad(jnp.transpose(target_points, (1, 2, 0)), ((0, 0), (0, 0), (0, 125)))
    return pl.pallas_call(
        near_body,
        out_shape=jax.ShapeDtypeStruct((leaf_count, RHS, CLUSTER), jnp.float32),
        in_specs=[
            pl.BlockSpec(memory_space=pltpu.SMEM),
            pl.BlockSpec(memory_space=pltpu.VMEM),
            pl.BlockSpec(memory_space=pltpu.VMEM),
        ],
        out_specs=pl.BlockSpec(memory_space=pltpu.VMEM),
    )(near_offsets, table, columns)


def mm(a, b):
    return jnp.matmul(a, b, precision=highest, preferred_element_type=jnp.float32)


def ordered(bit, own, other):
    return jnp.where(bit == 0, jnp.concatenate([own, other]), jnp.concatenate([other, own]))


def tree_field(root_coefficients, tree_up, tree_down, tree_coupling, me, first, second):
    up = tree_up[0].astype(jnp.float32).reshape(TOP_LEVELS, RANK, RANK)
    down = tree_down[0].astype(jnp.float32).reshape(TOP_LEVELS, RANK, RANK)
    cross = tree_coupling[0].astype(jnp.float32).reshape(TOP_LEVELS + 1, 4, RANK, RANK)
    eye = jnp.eye(RANK, dtype=jnp.float32)
    lift1 = up[0]
    lift2 = mm(lift1, up[1])
    lift3 = mm(lift2, up[2])
    lifts = jnp.stack([eye, lift1, lift2, lift3])
    push1 = down[0]
    push2 = mm(down[1], push1)
    push3 = mm(down[2], push2)
    pushes = jnp.stack([eye, push1, push2, push3])
    weights = jnp.einsum("sqkp,spm->sqkm", cross, pushes, precision=highest)

    p = jnp.einsum("rk,skq->srq", root_coefficients, lifts, precision=highest)

    bit0 = me & 1
    bit1 = (me >> 1) & 1
    bit2 = (me >> 2) & 1
    got1 = swap_with(p, 1)
    pairs0 = ordered(bit0, p[0:1], got1[0:1])
    coef1 = p[1] + got1[1]
    part2 = p[2] + got1[2]
    part3 = p[3] + got1[3]
    got2 = swap_with(jnp.concatenate([pairs0, coef1[None], part2[None], part3[None]]), 2)
    quads0 = ordered(bit1, pairs0, got2[0:2])
    pairs1 = ordered(bit1, coef1[None], got2[2:3])
    coef2 = part2 + got2[3]
    part3 = part3 + got2[4]
    got3 = swap_with(jnp.concatenate([quads0, pairs1, coef2[None], part3[None]]), 4)
    octs0 = ordered(bit2, quads0, got3[0:4])
    quads1 = ordered(bit2, pairs1, got3[4:6])
    pairs2 = ordered(bit2, coef2[None], got3[6:7])
    coef3 = (part3 + got3[7])[None]

    node = 8
    to_ahead = jnp.concatenate([octs0[5:8], quads1[1:4], pairs2, coef3])
    to_behind = jnp.concatenate([octs0[0:3], quads1[0:3], pairs2, coef3])
    to_ahead, to_behind, first = lax.optimization_barrier((to_ahead, to_behind, first))
    ahead1 = receive_from(to_behind, node)
    behind1 = receive_from(to_ahead, -node)
    to_behind = jnp.concatenate([pairs2[0:1], coef3, ahead1[8:9]])
    to_ahead = jnp.concatenate([pairs2[1:2], coef3, behind1[8:9]])
    to_ahead, to_behind, second = lax.optimization_barrier((to_ahead, to_behind, second))
    ahead2 = receive_from(to_behind, 2 * node)
    behind2 = receive_from(to_ahead, -2 * node)
    ahead3 = ahead2[2:3]
    behind3 = behind2[2:3]

    window0 = jnp.concatenate([behind1[0:3], octs0, ahead1[0:3]])
    window1 = jnp.concatenate([behind1[3:6], quads1, ahead1[3:6]])
    window2 = jnp.concatenate([behind2[0:1], behind1[6:8], pairs2, ahead1[6:8], ahead2[0:1]])
    steps = jnp.array(partner_steps, dtype=jnp.int32) + 3
    chosen0 = jnp.take(window0, (me & 7) + steps, axis=0, mode="clip")
    chosen1 = jnp.take(window1, ((me >> 1) & 3) + steps, axis=0, mode="clip")
    chosen2 = jnp.take(window2, bit2 + steps, axis=0, mode="clip")
    chosen3 = jnp.concatenate([behind3, behind2[1:2], ahead2[1:2], ahead3])
    chosen = jnp.stack([chosen0, chosen1, chosen2, chosen3])
    return jnp.einsum("sqrk,sqkm->rm", chosen, weights, precision=highest), first, second


def local(
    sources,
    points,
    near_offsets,
    far_offsets,
    source_basis,
    target_basis,
    leaf_coupling,
    leaf_up,
    leaf_down,
    tree_up,
    tree_down,
    tree_coupling,
):
    leaf_count = near_offsets.shape[0]
    n = device_count()
    me = lax.axis_index("leaf") * lax.axis_size("grp") + lax.axis_index("grp")
    leaf_values = sources.reshape(RHS, leaf_count, CLUSTER)
    leaf_coefficients = jnp.einsum(
        "rla,lak->lrk",
        leaf_values,
        source_basis.reshape(leaf_count, CLUSTER, RANK),
        preferred_element_type=jnp.float32,
    )
    coef_rows = leaf_coefficients.reshape(leaf_count, RHS * RANK)

    packed = jnp.concatenate([sources.astype(jnp.float32), points], axis=0)
    width = NEAR_REACH * CLUSTER
    to_right = jnp.concatenate(
        [packed[:, -width:].reshape(-1), coef_rows[-FAR_REACH:].reshape(-1)]
    )
    to_left = jnp.concatenate([packed[:, :width].reshape(-1), coef_rows[:FAR_REACH].reshape(-1)])
    from_left = lax.ppermute(to_right, AXES, [(i, i + 1) for i in range(n - 1)])
    from_right = lax.ppermute(to_left, AXES, [(i + 1, i) for i in range(n - 1)])
    split = (RHS + 3) * width
    extended = jnp.concatenate(
        [
            from_left[:split].reshape(RHS + 3, width),
            packed,
            from_right[:split].reshape(RHS + 3, width),
        ],
        axis=1,
    ).reshape(RHS + 3, leaf_count + 2 * NEAR_REACH, CLUSTER)
    rimmed = jnp.concatenate(
        [
            from_left[split:].reshape(FAR_REACH, RHS * RANK),
            coef_rows,
            from_right[split:].reshape(FAR_REACH, RHS * RANK),
        ]
    )

    target_points = points.reshape(3, leaf_count, CLUSTER)
    near_sum = near_field_kernel(extended, target_points, near_offsets)

    far_index = jnp.arange(leaf_count, dtype=jnp.int32)[:, None] + FAR_REACH + far_offsets
    partner_blocks = jnp.take(rimmed, far_index, axis=0).reshape(leaf_count, FAR_BLOCKS, RHS, RANK)
    leaf_far = jnp.einsum(
        "lfrk,lfkq->lrq",
        partner_blocks,
        leaf_coupling.reshape(leaf_count, FAR_BLOCKS, RANK, RANK),
        precision=bf16_weights,
        preferred_element_type=jnp.float32,
    )
    root_coefficients = jnp.einsum(
        "lrk,lkq->rq",
        leaf_coefficients,
        leaf_up.reshape(leaf_count, RANK, RANK),
        precision=bf16_weights,
        preferred_element_type=jnp.float32,
    )
    downward, near_sum, leaf_far = tree_field(
        root_coefficients, tree_up, tree_down, tree_coupling, me, near_sum, leaf_far
    )
    from_root = jnp.einsum(
        "rk,lkq->lrq",
        downward,
        leaf_down.reshape(leaf_count, RANK, RANK),
        precision=bf16_weights,
        preferred_element_type=jnp.float32,
    )
    leaf_field = leaf_far + from_root
    far_out = jnp.einsum(
        "lrk,lka->lra",
        leaf_field,
        target_basis.reshape(leaf_count, RANK, CLUSTER),
        precision=bf16_weights,
        preferred_element_type=jnp.float32,
    )
    product = jnp.transpose(near_sum + far_out, (1, 0, 2))
    return product.reshape(RHS, leaf_count * CLUSTER)


def solution(mesh):
    placed = (
        P(None, AXES),
        P(None, AXES),
        P(AXES, None),
        P(AXES, None),
        P(AXES, None),
        P(AXES, None),
        P(AXES, None, None),
        P(AXES, None),
        P(AXES, None),
        P(AXES, None, None),
        P(AXES, None, None),
        P(AXES, None, None, None),
    )
    return jax.shard_map(
        local, mesh=mesh, in_specs=placed, out_specs=P(None, AXES), check_vma=False
    )
```

```python
import jax
import jax.numpy as jnp
from jax import lax
from jax.experimental import pallas as pl
from jax.experimental.pallas import tpu as pltpu
from jax.sharding import PartitionSpec as P

CLUSTER = 64
RANK = 32
RHS = 16
NEAR_REACH = 16
NEAR_BLOCKS = 6
FAR_REACH = 32
FAR_BLOCKS = 8
TOP_LEVELS = 3


amplitude = 0.15
length_scale = 1.0
nugget = 0.5
partner_steps = (-3, -2, 2, 3)
highest = lax.Precision.HIGHEST
bf16_weights = lax.Precision.HIGH
AXES = ("leaf", "grp")


def device_count():
    return lax.axis_size("leaf") * lax.axis_size("grp")


def swap_with(value, mask):
    n = device_count()
    return lax.ppermute(value, AXES, [(i, i ^ mask) for i in range(n)])


def receive_from(value, step):
    n = device_count()
    return lax.ppermute(value, AXES, [(s, s - step) for s in range(n) if 0 <= s - step < n])


def near_body(offsets_ref, table_ref, columns_ref, out_ref):
    leaf_count = out_ref.shape[0]
    rows = RHS + 3
    lane = lax.broadcasted_iota(jnp.int32, (rows, 2 * CLUSTER), 1)
    low_half = lane < CLUSTER

    def one_leaf(i, carry):
        own = table_ref[i + NEAR_REACH]
        parts = []
        columns = columns_ref[i]
        for pair in range(NEAR_BLOCKS // 2):
            first = table_ref[i + NEAR_REACH + offsets_ref[i, 2 * pair]]
            second = table_ref[i + NEAR_REACH + offsets_ref[i, 2 * pair + 1]]
            joined = jnp.where(low_half, first, second)
            squared = None
            for component in range(3):
                separation = joined[RHS + component : RHS + component + 1, :] - columns[:, component : component + 1]
                term = separation * separation
                squared = term if squared is None else squared + term
            kernel = (amplitude * jnp.exp(-jnp.sqrt(squared) / length_scale)).astype(jnp.bfloat16)
            values = joined[:RHS].astype(jnp.bfloat16)
            parts.append(
                lax.dot_general(
                    values, kernel, (((1,), (1,)), ((), ())), preferred_element_type=jnp.float32
                )
            )
        out_ref[i] = nugget * own[:RHS, :CLUSTER] + (parts[0] + parts[1] + parts[2])
        return carry

    lax.fori_loop(0, leaf_count, one_leaf, 0, unroll=16)


def near_field_kernel(extended, target_points, near_offsets):
    leaf_count = target_points.shape[1]
    by_leaf = jnp.transpose(extended, (1, 0, 2))
    table = jnp.concatenate([by_leaf, by_leaf], axis=2)
    columns = jnp.pad(jnp.transpose(target_points, (1, 2, 0)), ((0, 0), (0, 0), (0, 125)))
    return pl.pallas_call(
        near_body,
        out_shape=jax.ShapeDtypeStruct((leaf_count, RHS, CLUSTER), jnp.float32),
        in_specs=[
            pl.BlockSpec(memory_space=pltpu.SMEM),
            pl.BlockSpec(memory_space=pltpu.VMEM),
            pl.BlockSpec(memory_space=pltpu.VMEM),
        ],
        out_specs=pl.BlockSpec(memory_space=pltpu.VMEM),
    )(near_offsets, table, columns)


def mm(a, b):
    return jnp.matmul(a, b, precision=highest, preferred_element_type=jnp.float32)


def ordered(bit, own, other):
    return jnp.where(bit == 0, jnp.concatenate([own, other]), jnp.concatenate([other, own]))


def tree_weights(tree_up, tree_down, tree_coupling):
    up = tree_up[0].astype(jnp.float32).reshape(TOP_LEVELS, RANK, RANK)
    down = tree_down[0].astype(jnp.float32).reshape(TOP_LEVELS, RANK, RANK)
    cross = tree_coupling[0].astype(jnp.float32).reshape(TOP_LEVELS + 1, 4, RANK, RANK)
    eye = jnp.eye(RANK, dtype=jnp.float32)
    lift1 = up[0]
    lift2 = mm(lift1, up[1])
    lift3 = mm(lift2, up[2])
    lifts = jnp.stack([eye, lift1, lift2, lift3])
    push1 = down[0]
    push2 = mm(down[1], push1)
    push3 = mm(down[2], push2)
    pushes = jnp.stack([eye, push1, push2, push3])
    weights = jnp.einsum("sqkp,spm->sqkm", cross, pushes, precision=highest)
    return lifts, weights


def tree_field(p, partner_p, weights, me, first, second):
    bit0 = me & 1
    pair = (me >> 1) & 3
    bit2 = (me >> 2) & 1
    pairs0 = ordered(bit0, p[0:1], partner_p[0:1])
    summed = p[1:4] + partner_p[1:4]
    mine = jnp.concatenate([pairs0, summed])
    held = jnp.stack([mine, swap_with(mine, 2), swap_with(mine, 4), swap_with(mine, 6)])
    node_pairs = jnp.take(held, pair ^ jnp.arange(4, dtype=jnp.int32), axis=0, mode="clip")
    octs0 = node_pairs[:, 0:2].reshape(8, RHS, RANK)
    quads1 = node_pairs[:, 2]
    pairs2 = node_pairs[0::2, 3] + node_pairs[1::2, 3]
    coef3 = jnp.sum(node_pairs[:, 4], axis=0)[None]

    node = 8
    to_ahead = jnp.concatenate([octs0[5:8], quads1[1:4], pairs2, coef3])
    to_behind = jnp.concatenate([octs0[0:3], quads1[0:3], pairs2, coef3])
    to_ahead, to_behind, first = lax.optimization_barrier((to_ahead, to_behind, first))
    ahead1 = receive_from(to_behind, node)
    behind1 = receive_from(to_ahead, -node)
    to_behind = jnp.concatenate([pairs2[0:1], coef3, ahead1[8:9]])
    to_ahead = jnp.concatenate([pairs2[1:2], coef3, behind1[8:9]])
    to_ahead, to_behind, second = lax.optimization_barrier((to_ahead, to_behind, second))
    ahead2 = receive_from(to_behind, 2 * node)
    behind2 = receive_from(to_ahead, -2 * node)
    ahead3 = ahead2[2:3]
    behind3 = behind2[2:3]

    window0 = jnp.concatenate([behind1[0:3], octs0, ahead1[0:3]])
    window1 = jnp.concatenate([behind1[3:6], quads1, ahead1[3:6]])
    window2 = jnp.concatenate([behind2[0:1], behind1[6:8], pairs2, ahead1[6:8], ahead2[0:1]])
    steps = jnp.array(partner_steps, dtype=jnp.int32) + 3
    chosen0 = jnp.take(window0, (me & 7) + steps, axis=0, mode="clip")
    chosen1 = jnp.take(window1, pair + steps, axis=0, mode="clip")
    chosen2 = jnp.take(window2, bit2 + steps, axis=0, mode="clip")
    chosen3 = jnp.concatenate([behind3, behind2[1:2], ahead2[1:2], ahead3])
    chosen = jnp.stack([chosen0, chosen1, chosen2, chosen3])
    return jnp.einsum("sqrk,sqkm->rm", chosen, weights, precision=highest), first, second


def local(
    sources,
    points,
    near_offsets,
    far_offsets,
    source_basis,
    target_basis,
    leaf_coupling,
    leaf_up,
    leaf_down,
    tree_up,
    tree_down,
    tree_coupling,
):
    leaf_count = near_offsets.shape[0]
    n = device_count()
    me = lax.axis_index("leaf") * lax.axis_size("grp") + lax.axis_index("grp")
    leaf_values = sources.reshape(RHS, leaf_count, CLUSTER)
    leaf_coefficients = jnp.einsum(
        "rla,lak->lrk",
        leaf_values,
        source_basis.reshape(leaf_count, CLUSTER, RANK),
        preferred_element_type=jnp.float32,
    )
    coef_rows = leaf_coefficients.reshape(leaf_count, RHS * RANK)

    root_coefficients = jnp.einsum(
        "lrk,lkq->rq",
        leaf_coefficients,
        leaf_up.reshape(leaf_count, RANK, RANK),
        precision=bf16_weights,
        preferred_element_type=jnp.float32,
    )
    lifts, weights = tree_weights(tree_up, tree_down, tree_coupling)
    p = jnp.einsum("rk,skq->srq", root_coefficients, lifts, precision=highest)

    packed = jnp.concatenate([sources.astype(jnp.float32), points], axis=0)
    width = NEAR_REACH * CLUSTER
    to_right = jnp.concatenate(
        [packed[:, -width:].reshape(-1), coef_rows[-FAR_REACH:].reshape(-1), p.reshape(-1)]
    )
    to_left = jnp.concatenate(
        [packed[:, :width].reshape(-1), coef_rows[:FAR_REACH].reshape(-1), p.reshape(-1)]
    )
    from_left = lax.ppermute(to_right, AXES, [(i, i + 1) for i in range(n - 1)])
    from_right = lax.ppermute(to_left, AXES, [(i + 1, i) for i in range(n - 1)])
    split = (RHS + 3) * width
    split2 = split + FAR_REACH * RHS * RANK
    partner_p = jnp.where(
        (me & 1) == 0, from_right[split2:], from_left[split2:]
    ).reshape(TOP_LEVELS + 1, RHS, RANK)
    extended = jnp.concatenate(
        [
            from_left[:split].reshape(RHS + 3, width),
            packed,
            from_right[:split].reshape(RHS + 3, width),
        ],
        axis=1,
    ).reshape(RHS + 3, leaf_count + 2 * NEAR_REACH, CLUSTER)
    rimmed = jnp.concatenate(
        [
            from_left[split:split2].reshape(FAR_REACH, RHS * RANK),
            coef_rows,
            from_right[split:split2].reshape(FAR_REACH, RHS * RANK),
        ]
    )

    target_points = points.reshape(3, leaf_count, CLUSTER)
    near_sum = near_field_kernel(extended, target_points, near_offsets)

    far_index = jnp.arange(leaf_count, dtype=jnp.int32)[:, None] + FAR_REACH + far_offsets
    partner_blocks = jnp.take(rimmed, far_index, axis=0).reshape(leaf_count, FAR_BLOCKS, RHS, RANK)
    leaf_far = jnp.einsum(
        "lfrk,lfkq->lrq",
        partner_blocks,
        leaf_coupling.reshape(leaf_count, FAR_BLOCKS, RANK, RANK),
        precision=bf16_weights,
        preferred_element_type=jnp.float32,
    )
    downward, near_sum, leaf_far = tree_field(p, partner_p, weights, me, near_sum, leaf_far)
    from_root = jnp.einsum(
        "rk,lkq->lrq",
        downward,
        leaf_down.reshape(leaf_count, RANK, RANK),
        precision=bf16_weights,
        preferred_element_type=jnp.float32,
    )
    leaf_field = leaf_far + from_root
    far_out = jnp.einsum(
        "lrk,lka->lra",
        leaf_field,
        target_basis.reshape(leaf_count, RANK, CLUSTER),
        precision=bf16_weights,
        preferred_element_type=jnp.float32,
    )
    product = jnp.transpose(near_sum + far_out, (1, 0, 2))
    return product.reshape(RHS, leaf_count * CLUSTER)


def solution(mesh):
    placed = (
        P(None, AXES),
        P(None, AXES),
        P(AXES, None),
        P(AXES, None),
        P(AXES, None),
        P(AXES, None),
        P(AXES, None, None),
        P(AXES, None),
        P(AXES, None),
        P(AXES, None, None),
        P(AXES, None, None),
        P(AXES, None, None, None),
    )
    return jax.shard_map(
        local, mesh=mesh, in_specs=placed, out_specs=P(None, AXES), check_vma=False
    )
```

```python
import jax
import jax.numpy as jnp
from jax import lax
from jax.experimental import pallas as pl
from jax.experimental.pallas import tpu as pltpu
from jax.sharding import PartitionSpec as P

CLUSTER = 64
RANK = 32
RHS = 16
NEAR_REACH = 16
NEAR_BLOCKS = 6
FAR_REACH = 32
FAR_BLOCKS = 8
TOP_LEVELS = 3


amplitude = 0.15
length_scale = 1.0
nugget = 0.5
partner_steps = (-3, -2, 2, 3)
highest = lax.Precision.HIGHEST
bf16_weights = lax.Precision.HIGH
AXES = ("leaf", "grp")


def device_count():
    return lax.axis_size("leaf") * lax.axis_size("grp")


def swap_with(value, mask):
    n = device_count()
    return lax.ppermute(value, AXES, [(i, i ^ mask) for i in range(n)])


def receive_from(value, step):
    n = device_count()
    return lax.ppermute(value, AXES, [(s, s - step) for s in range(n) if 0 <= s - step < n])


def near_body(offsets_ref, table_ref, columns_ref, out_ref):
    leaf_count = out_ref.shape[0]
    rows = RHS + 3
    lane = lax.broadcasted_iota(jnp.int32, (rows, 2 * CLUSTER), 1)
    low_half = lane < CLUSTER

    def one_leaf(i, carry):
        own = table_ref[i + NEAR_REACH]
        parts = []
        columns = columns_ref[i]
        for pair in range(NEAR_BLOCKS // 2):
            first = table_ref[i + NEAR_REACH + offsets_ref[i, 2 * pair]]
            second = table_ref[i + NEAR_REACH + offsets_ref[i, 2 * pair + 1]]
            joined = jnp.where(low_half, first, second)
            squared = None
            for component in range(3):
                separation = joined[RHS + component : RHS + component + 1, :] - columns[:, component : component + 1]
                term = separation * separation
                squared = term if squared is None else squared + term
            kernel = (amplitude * jnp.exp(-jnp.sqrt(squared) / length_scale)).astype(jnp.bfloat16)
            values = joined[:RHS].astype(jnp.bfloat16)
            parts.append(
                lax.dot_general(
                    values, kernel, (((1,), (1,)), ((), ())), preferred_element_type=jnp.float32
                )
            )
        out_ref[i] = nugget * own[:RHS, :CLUSTER] + (parts[0] + parts[1] + parts[2])
        return carry

    lax.fori_loop(0, leaf_count, one_leaf, 0, unroll=16)


def near_field_kernel(extended, target_points, near_offsets):
    leaf_count = target_points.shape[1]
    by_leaf = jnp.transpose(extended, (1, 0, 2))
    table = jnp.concatenate([by_leaf, by_leaf], axis=2)
    columns = jnp.pad(jnp.transpose(target_points, (1, 2, 0)), ((0, 0), (0, 0), (0, 125)))
    return pl.pallas_call(
        near_body,
        out_shape=jax.ShapeDtypeStruct((leaf_count, RHS, CLUSTER), jnp.float32),
        in_specs=[
            pl.BlockSpec(memory_space=pltpu.SMEM),
            pl.BlockSpec(memory_space=pltpu.VMEM),
            pl.BlockSpec(memory_space=pltpu.VMEM),
        ],
        out_specs=pl.BlockSpec(memory_space=pltpu.VMEM),
    )(near_offsets, table, columns)


def mm(a, b):
    return jnp.matmul(a, b, precision=highest, preferred_element_type=jnp.float32)


def ordered(bit, own, other):
    return jnp.where(bit == 0, jnp.concatenate([own, other]), jnp.concatenate([other, own]))


def tree_field(root_coefficients, tree_up, tree_down, tree_coupling, me, first, second):
    up = tree_up[0].astype(jnp.float32).reshape(TOP_LEVELS, RANK, RANK)
    down = tree_down[0].astype(jnp.float32).reshape(TOP_LEVELS, RANK, RANK)
    cross = tree_coupling[0].astype(jnp.float32).reshape(TOP_LEVELS + 1, 4, RANK, RANK)
    eye = jnp.eye(RANK, dtype=jnp.float32)
    lift1 = up[0]
    lift2 = mm(lift1, up[1])
    lift3 = mm(lift2, up[2])
    lifts = jnp.stack([eye, lift1, lift2, lift3])
    push1 = down[0]
    push2 = mm(down[1], push1)
    push3 = mm(down[2], push2)
    pushes = jnp.stack([eye, push1, push2, push3])
    weights = jnp.einsum("sqkp,spm->sqkm", cross, pushes, precision=highest)

    p = jnp.einsum("rk,skq->srq", root_coefficients, lifts, precision=highest)

    bit0 = me & 1
    bit1 = (me >> 1) & 1
    bit2 = (me >> 2) & 1
    got1 = swap_with(p, 1)
    pairs0 = ordered(bit0, p[0:1], got1[0:1])
    coef1 = p[1] + got1[1]
    part2 = p[2] + got1[2]
    part3 = p[3] + got1[3]
    got2 = swap_with(jnp.concatenate([pairs0, coef1[None], part2[None], part3[None]]), 2)
    quads0 = ordered(bit1, pairs0, got2[0:2])
    pairs1 = ordered(bit1, coef1[None], got2[2:3])
    coef2 = part2 + got2[3]
    part3 = part3 + got2[4]
    got3 = swap_with(jnp.concatenate([quads0, pairs1, coef2[None], part3[None]]), 4)
    octs0 = ordered(bit2, quads0, got3[0:4])
    quads1 = ordered(bit2, pairs1, got3[4:6])
    pairs2 = ordered(bit2, coef2[None], got3[6:7])
    coef3 = (part3 + got3[7])[None]

    node = 8
    to_ahead = jnp.concatenate([octs0[5:8], quads1[1:4], pairs2])
    to_behind = jnp.concatenate([octs0[0:3], quads1[0:3], pairs2])
    far_ahead = jnp.concatenate([pairs2[1:2], coef3])
    far_behind = jnp.concatenate([pairs2[0:1], coef3])
    to_ahead, to_behind, far_ahead, far_behind, first = lax.optimization_barrier(
        (to_ahead, to_behind, far_ahead, far_behind, first)
    )
    ahead1 = receive_from(to_behind, node)
    behind1 = receive_from(to_ahead, -node)
    ahead2 = receive_from(far_behind, 2 * node)
    behind2 = receive_from(far_ahead, -2 * node)
    ahead3 = receive_from(far_behind[1:2], 3 * node)
    behind3 = receive_from(far_ahead[1:2], -3 * node)

    window0 = jnp.concatenate([behind1[0:3], octs0, ahead1[0:3]])
    window1 = jnp.concatenate([behind1[3:6], quads1, ahead1[3:6]])
    window2 = jnp.concatenate([behind2[0:1], behind1[6:8], pairs2, ahead1[6:8], ahead2[0:1]])
    steps = jnp.array(partner_steps, dtype=jnp.int32) + 3
    chosen0 = jnp.take(window0, (me & 7) + steps, axis=0, mode="clip")
    chosen1 = jnp.take(window1, ((me >> 1) & 3) + steps, axis=0, mode="clip")
    chosen2 = jnp.take(window2, bit2 + steps, axis=0, mode="clip")
    chosen3 = jnp.concatenate([behind3, behind2[1:2], ahead2[1:2], ahead3])
    chosen = jnp.stack([chosen0, chosen1, chosen2, chosen3])
    return jnp.einsum("sqrk,sqkm->rm", chosen, weights, precision=highest), first, second


def local(
    sources,
    points,
    near_offsets,
    far_offsets,
    source_basis,
    target_basis,
    leaf_coupling,
    leaf_up,
    leaf_down,
    tree_up,
    tree_down,
    tree_coupling,
):
    leaf_count = near_offsets.shape[0]
    n = device_count()
    me = lax.axis_index("leaf") * lax.axis_size("grp") + lax.axis_index("grp")
    leaf_values = sources.reshape(RHS, leaf_count, CLUSTER)
    leaf_coefficients = jnp.einsum(
        "rla,lak->lrk",
        leaf_values,
        source_basis.reshape(leaf_count, CLUSTER, RANK),
        preferred_element_type=jnp.float32,
    )
    coef_rows = leaf_coefficients.reshape(leaf_count, RHS * RANK)

    packed = jnp.concatenate([sources.astype(jnp.float32), points], axis=0)
    width = NEAR_REACH * CLUSTER
    to_right = jnp.concatenate(
        [packed[:, -width:].reshape(-1), coef_rows[-FAR_REACH:].reshape(-1)]
    )
    to_left = jnp.concatenate([packed[:, :width].reshape(-1), coef_rows[:FAR_REACH].reshape(-1)])
    from_left = lax.ppermute(to_right, AXES, [(i, i + 1) for i in range(n - 1)])
    from_right = lax.ppermute(to_left, AXES, [(i + 1, i) for i in range(n - 1)])
    split = (RHS + 3) * width
    extended = jnp.concatenate(
        [
            from_left[:split].reshape(RHS + 3, width),
            packed,
            from_right[:split].reshape(RHS + 3, width),
        ],
        axis=1,
    ).reshape(RHS + 3, leaf_count + 2 * NEAR_REACH, CLUSTER)
    rimmed = jnp.concatenate(
        [
            from_left[split:].reshape(FAR_REACH, RHS * RANK),
            coef_rows,
            from_right[split:].reshape(FAR_REACH, RHS * RANK),
        ]
    )

    target_points = points.reshape(3, leaf_count, CLUSTER)
    near_sum = near_field_kernel(extended, target_points, near_offsets)

    far_index = jnp.arange(leaf_count, dtype=jnp.int32)[:, None] + FAR_REACH + far_offsets
    partner_blocks = jnp.take(rimmed, far_index, axis=0).reshape(leaf_count, FAR_BLOCKS, RHS, RANK)
    leaf_far = jnp.einsum(
        "lfrk,lfkq->lrq",
        partner_blocks,
        leaf_coupling.reshape(leaf_count, FAR_BLOCKS, RANK, RANK),
        precision=bf16_weights,
        preferred_element_type=jnp.float32,
    )
    root_coefficients = jnp.einsum(
        "lrk,lkq->rq",
        leaf_coefficients,
        leaf_up.reshape(leaf_count, RANK, RANK),
        precision=bf16_weights,
        preferred_element_type=jnp.float32,
    )
    downward, near_sum, leaf_far = tree_field(
        root_coefficients, tree_up, tree_down, tree_coupling, me, near_sum, leaf_far
    )
    from_root = jnp.einsum(
        "rk,lkq->lrq",
        downward,
        leaf_down.reshape(leaf_count, RANK, RANK),
        precision=bf16_weights,
        preferred_element_type=jnp.float32,
    )
    leaf_field = leaf_far + from_root
    far_out = jnp.einsum(
        "lrk,lka->lra",
        leaf_field,
        target_basis.reshape(leaf_count, RANK, CLUSTER),
        precision=bf16_weights,
        preferred_element_type=jnp.float32,
    )
    product = jnp.transpose(near_sum + far_out, (1, 0, 2))
    return product.reshape(RHS, leaf_count * CLUSTER)


def solution(mesh):
    placed = (
        P(None, AXES),
        P(None, AXES),
        P(AXES, None),
        P(AXES, None),
        P(AXES, None),
        P(AXES, None),
        P(AXES, None, None),
        P(AXES, None),
        P(AXES, None),
        P(AXES, None, None),
        P(AXES, None, None),
        P(AXES, None, None, None),
    )
    return jax.shard_map(
        local, mesh=mesh, in_specs=placed, out_specs=P(None, AXES), check_vma=False
    )
```

```python
import jax
import jax.numpy as jnp
from jax import lax
from jax.experimental import pallas as pl
from jax.experimental.pallas import tpu as pltpu
from jax.sharding import PartitionSpec as P

CLUSTER = 64
RANK = 32
RHS = 16
NEAR_REACH = 16
NEAR_BLOCKS = 6
FAR_REACH = 32
FAR_BLOCKS = 8
TOP_LEVELS = 3


amplitude = 0.15
length_scale = 1.0
nugget = 0.5
partner_steps = (-3, -2, 2, 3)
highest = lax.Precision.HIGHEST
bf16_weights = lax.Precision.HIGH
AXES = ("leaf", "grp")


def device_count():
    return lax.axis_size("leaf") * lax.axis_size("grp")


def swap_with(value, mask):
    n = device_count()
    return lax.ppermute(value, AXES, [(i, i ^ mask) for i in range(n)])


def receive_from(value, step):
    n = device_count()
    return lax.ppermute(value, AXES, [(s, s - step) for s in range(n) if 0 <= s - step < n])


def near_body(offsets_ref, table_ref, columns_ref, out_ref):
    leaf_count = out_ref.shape[0]
    rows = RHS + 3
    lane = lax.broadcasted_iota(jnp.int32, (rows, 2 * CLUSTER), 1)
    low_half = lane < CLUSTER

    def one_leaf(i, carry):
        own = table_ref[i + NEAR_REACH]
        parts = []
        columns = jnp.transpose(columns_ref[i])[:CLUSTER]
        for pair in range(NEAR_BLOCKS // 2):
            first = table_ref[i + NEAR_REACH + offsets_ref[i, 2 * pair]]
            second = table_ref[i + NEAR_REACH + offsets_ref[i, 2 * pair + 1]]
            joined = jnp.where(low_half, first, second)
            squared = None
            for component in range(3):
                separation = joined[RHS + component : RHS + component + 1, :] - columns[:, component : component + 1]
                term = separation * separation
                squared = term if squared is None else squared + term
            kernel = (amplitude * jnp.exp(-jnp.sqrt(squared) / length_scale)).astype(jnp.bfloat16)
            values = joined[:RHS].astype(jnp.bfloat16)
            parts.append(
                lax.dot_general(
                    values, kernel, (((1,), (1,)), ((), ())), preferred_element_type=jnp.float32
                )
            )
        out_ref[i] = nugget * own[:RHS, :CLUSTER] + (parts[0] + parts[1] + parts[2])
        return carry

    lax.fori_loop(0, leaf_count, one_leaf, 0, unroll=16)


def near_field_kernel(extended, target_points, near_offsets):
    leaf_count = target_points.shape[1]
    by_leaf = jnp.transpose(extended, (1, 0, 2))
    table = jnp.concatenate([by_leaf, by_leaf], axis=2)
    columns = jnp.pad(jnp.transpose(target_points, (1, 0, 2)), ((0, 0), (0, 5), (0, CLUSTER)))
    return pl.pallas_call(
        near_body,
        out_shape=jax.ShapeDtypeStruct((leaf_count, RHS, CLUSTER), jnp.float32),
        in_specs=[
            pl.BlockSpec(memory_space=pltpu.SMEM),
            pl.BlockSpec(memory_space=pltpu.VMEM),
            pl.BlockSpec(memory_space=pltpu.VMEM),
        ],
        out_specs=pl.BlockSpec(memory_space=pltpu.VMEM),
    )(near_offsets, table, columns)


def mm(a, b):
    return jnp.matmul(a, b, precision=highest, preferred_element_type=jnp.float32)


def ordered(bit, own, other):
    return jnp.where(bit == 0, jnp.concatenate([own, other]), jnp.concatenate([other, own]))


def tree_field(root_coefficients, tree_up, tree_down, tree_coupling, me, first, second):
    up = tree_up[0].astype(jnp.float32).reshape(TOP_LEVELS, RANK, RANK)
    down = tree_down[0].astype(jnp.float32).reshape(TOP_LEVELS, RANK, RANK)
    cross = tree_coupling[0].astype(jnp.float32).reshape(TOP_LEVELS + 1, 4, RANK, RANK)
    eye = jnp.eye(RANK, dtype=jnp.float32)
    lift1 = up[0]
    lift2 = mm(lift1, up[1])
    lift3 = mm(lift2, up[2])
    lifts = jnp.stack([eye, lift1, lift2, lift3])
    push1 = down[0]
    push2 = mm(down[1], push1)
    push3 = mm(down[2], push2)
    pushes = jnp.stack([eye, push1, push2, push3])
    weights = jnp.einsum("sqkp,spm->sqkm", cross, pushes, precision=highest)

    p = jnp.einsum("rk,skq->srq", root_coefficients, lifts, precision=highest)

    bit0 = me & 1
    bit1 = (me >> 1) & 1
    bit2 = (me >> 2) & 1
    got1 = swap_with(p, 1)
    pairs0 = ordered(bit0, p[0:1], got1[0:1])
    coef1 = p[1] + got1[1]
    part2 = p[2] + got1[2]
    part3 = p[3] + got1[3]
    got2 = swap_with(jnp.concatenate([pairs0, coef1[None], part2[None], part3[None]]), 2)
    quads0 = ordered(bit1, pairs0, got2[0:2])
    pairs1 = ordered(bit1, coef1[None], got2[2:3])
    coef2 = part2 + got2[3]
    part3 = part3 + got2[4]
    got3 = swap_with(jnp.concatenate([quads0, pairs1, coef2[None], part3[None]]), 4)
    octs0 = ordered(bit2, quads0, got3[0:4])
    quads1 = ordered(bit2, pairs1, got3[4:6])
    pairs2 = ordered(bit2, coef2[None], got3[6:7])
    coef3 = (part3 + got3[7])[None]

    node = 8
    to_ahead = jnp.concatenate([octs0[5:8], quads1[1:4], pairs2, coef3])
    to_behind = jnp.concatenate([octs0[0:3], quads1[0:3], pairs2, coef3])
    to_ahead, to_behind, first = lax.optimization_barrier((to_ahead, to_behind, first))
    ahead1 = receive_from(to_behind, node)
    behind1 = receive_from(to_ahead, -node)
    to_behind = jnp.concatenate([pairs2[0:1], coef3, ahead1[8:9]])
    to_ahead = jnp.concatenate([pairs2[1:2], coef3, behind1[8:9]])
    to_ahead, to_behind, second = lax.optimization_barrier((to_ahead, to_behind, second))
    ahead2 = receive_from(to_behind, 2 * node)
    behind2 = receive_from(to_ahead, -2 * node)
    ahead3 = ahead2[2:3]
    behind3 = behind2[2:3]

    window0 = jnp.concatenate([behind1[0:3], octs0, ahead1[0:3]])
    window1 = jnp.concatenate([behind1[3:6], quads1, ahead1[3:6]])
    window2 = jnp.concatenate([behind2[0:1], behind1[6:8], pairs2, ahead1[6:8], ahead2[0:1]])
    steps = jnp.array(partner_steps, dtype=jnp.int32) + 3
    chosen0 = jnp.take(window0, (me & 7) + steps, axis=0, mode="clip")
    chosen1 = jnp.take(window1, ((me >> 1) & 3) + steps, axis=0, mode="clip")
    chosen2 = jnp.take(window2, bit2 + steps, axis=0, mode="clip")
    chosen3 = jnp.concatenate([behind3, behind2[1:2], ahead2[1:2], ahead3])
    chosen = jnp.stack([chosen0, chosen1, chosen2, chosen3])
    return jnp.einsum("sqrk,sqkm->rm", chosen, weights, precision=highest), first, second


def local(
    sources,
    points,
    near_offsets,
    far_offsets,
    source_basis,
    target_basis,
    leaf_coupling,
    leaf_up,
    leaf_down,
    tree_up,
    tree_down,
    tree_coupling,
):
    leaf_count = near_offsets.shape[0]
    n = device_count()
    me = lax.axis_index("leaf") * lax.axis_size("grp") + lax.axis_index("grp")
    leaf_values = sources.reshape(RHS, leaf_count, CLUSTER)
    leaf_coefficients = jnp.einsum(
        "rla,lak->lrk",
        leaf_values,
        source_basis.reshape(leaf_count, CLUSTER, RANK),
        preferred_element_type=jnp.float32,
    )
    coef_rows = leaf_coefficients.reshape(leaf_count, RHS * RANK)

    packed = jnp.concatenate([sources.astype(jnp.float32), points], axis=0)
    width = NEAR_REACH * CLUSTER
    to_right = jnp.concatenate(
        [packed[:, -width:].reshape(-1), coef_rows[-FAR_REACH:].reshape(-1)]
    )
    to_left = jnp.concatenate([packed[:, :width].reshape(-1), coef_rows[:FAR_REACH].reshape(-1)])
    from_left = lax.ppermute(to_right, AXES, [(i, i + 1) for i in range(n - 1)])
    from_right = lax.ppermute(to_left, AXES, [(i + 1, i) for i in range(n - 1)])
    split = (RHS + 3) * width
    extended = jnp.concatenate(
        [
            from_left[:split].reshape(RHS + 3, width),
            packed,
            from_right[:split].reshape(RHS + 3, width),
        ],
        axis=1,
    ).reshape(RHS + 3, leaf_count + 2 * NEAR_REACH, CLUSTER)
    rimmed = jnp.concatenate(
        [
            from_left[split:].reshape(FAR_REACH, RHS * RANK),
            coef_rows,
            from_right[split:].reshape(FAR_REACH, RHS * RANK),
        ]
    )

    target_points = points.reshape(3, leaf_count, CLUSTER)
    near_sum = near_field_kernel(extended, target_points, near_offsets)

    far_index = jnp.arange(leaf_count, dtype=jnp.int32)[:, None] + FAR_REACH + far_offsets
    partner_blocks = jnp.take(rimmed, far_index, axis=0).reshape(leaf_count, FAR_BLOCKS, RHS, RANK)
    leaf_far = jnp.einsum(
        "lfrk,lfkq->lrq",
        partner_blocks,
        leaf_coupling.reshape(leaf_count, FAR_BLOCKS, RANK, RANK),
        precision=bf16_weights,
        preferred_element_type=jnp.float32,
    )
    root_coefficients = jnp.einsum(
        "lrk,lkq->rq",
        leaf_coefficients,
        leaf_up.reshape(leaf_count, RANK, RANK),
        precision=bf16_weights,
        preferred_element_type=jnp.float32,
    )
    downward, near_sum, leaf_far = tree_field(
        root_coefficients, tree_up, tree_down, tree_coupling, me, near_sum, leaf_far
    )
    from_root = jnp.einsum(
        "rk,lkq->lrq",
        downward,
        leaf_down.reshape(leaf_count, RANK, RANK),
        precision=bf16_weights,
        preferred_element_type=jnp.float32,
    )
    leaf_field = leaf_far + from_root
    far_out = jnp.einsum(
        "lrk,lka->lra",
        leaf_field,
        target_basis.reshape(leaf_count, RANK, CLUSTER),
        precision=bf16_weights,
        preferred_element_type=jnp.float32,
    )
    product = jnp.transpose(near_sum + far_out, (1, 0, 2))
    return product.reshape(RHS, leaf_count * CLUSTER)


def solution(mesh):
    placed = (
        P(None, AXES),
        P(None, AXES),
        P(AXES, None),
        P(AXES, None),
        P(AXES, None),
        P(AXES, None),
        P(AXES, None, None),
        P(AXES, None),
        P(AXES, None),
        P(AXES, None, None),
        P(AXES, None, None),
        P(AXES, None, None, None),
    )
    return jax.shard_map(
        local, mesh=mesh, in_specs=placed, out_specs=P(None, AXES), check_vma=False
    )
```

```python
import jax
import jax.numpy as jnp
from jax import lax
from jax.experimental import pallas as pl
from jax.experimental.pallas import tpu as pltpu
from jax.sharding import PartitionSpec as P

CLUSTER = 64
RANK = 32
RHS = 16
NEAR_REACH = 16
NEAR_BLOCKS = 6
FAR_REACH = 32
FAR_BLOCKS = 8
TOP_LEVELS = 3


amplitude = 0.15
length_scale = 1.0
nugget = 0.5
partner_steps = (-3, -2, 2, 3)
highest = lax.Precision.HIGHEST
bf16_weights = lax.Precision.HIGH
AXES = ("leaf", "grp")


def device_count():
    return lax.axis_size("leaf") * lax.axis_size("grp")


def swap_with(value, mask):
    n = device_count()
    return lax.ppermute(value, AXES, [(i, i ^ mask) for i in range(n)])


def receive_from(value, step):
    n = device_count()
    return lax.ppermute(value, AXES, [(s, s - step) for s in range(n) if 0 <= s - step < n])


def near_body(offsets_ref, table_ref, columns_ref, out_ref):
    leaf_count = out_ref.shape[0]
    rows = RHS + 3

    def one_leaf(i, carry):
        own = table_ref[i + NEAR_REACH]
        parts = []
        columns = jnp.transpose(columns_ref[i])[:CLUSTER]
        for pair in range(NEAR_BLOCKS // 2):
            first = table_ref[i + NEAR_REACH + offsets_ref[i, 2 * pair]]
            second = table_ref[i + NEAR_REACH + offsets_ref[i, 2 * pair + 1]]
            joined = jnp.concatenate([first, second], axis=1)
            squared = None
            for component in range(3):
                separation = joined[RHS + component : RHS + component + 1, :] - columns[:, component : component + 1]
                term = separation * separation
                squared = term if squared is None else squared + term
            kernel = (amplitude * jnp.exp(-jnp.sqrt(squared) / length_scale)).astype(jnp.bfloat16)
            values = joined[:RHS].astype(jnp.bfloat16)
            parts.append(
                lax.dot_general(
                    values, kernel, (((1,), (1,)), ((), ())), preferred_element_type=jnp.float32
                )
            )
        out_ref[i] = nugget * own[:RHS] + (parts[0] + parts[1] + parts[2])
        return carry

    lax.fori_loop(0, leaf_count, one_leaf, 0, unroll=16)


def near_field_kernel(extended, target_points, near_offsets):
    leaf_count = target_points.shape[1]
    by_leaf = jnp.transpose(extended, (1, 0, 2))
    table = by_leaf
    columns = jnp.pad(jnp.transpose(target_points, (1, 0, 2)), ((0, 0), (0, 5), (0, CLUSTER)))
    return pl.pallas_call(
        near_body,
        out_shape=jax.ShapeDtypeStruct((leaf_count, RHS, CLUSTER), jnp.float32),
        in_specs=[
            pl.BlockSpec(memory_space=pltpu.SMEM),
            pl.BlockSpec(memory_space=pltpu.VMEM),
            pl.BlockSpec(memory_space=pltpu.VMEM),
        ],
        out_specs=pl.BlockSpec(memory_space=pltpu.VMEM),
    )(near_offsets, table, columns)


def mm(a, b):
    return jnp.matmul(a, b, precision=highest, preferred_element_type=jnp.float32)


def ordered(bit, own, other):
    return jnp.where(bit == 0, jnp.concatenate([own, other]), jnp.concatenate([other, own]))


def tree_field(root_coefficients, tree_up, tree_down, tree_coupling, me, first, second):
    up = tree_up[0].astype(jnp.float32).reshape(TOP_LEVELS, RANK, RANK)
    down = tree_down[0].astype(jnp.float32).reshape(TOP_LEVELS, RANK, RANK)
    cross = tree_coupling[0].astype(jnp.float32).reshape(TOP_LEVELS + 1, 4, RANK, RANK)
    eye = jnp.eye(RANK, dtype=jnp.float32)
    lift1 = up[0]
    lift2 = mm(lift1, up[1])
    lift3 = mm(lift2, up[2])
    lifts = jnp.stack([eye, lift1, lift2, lift3])
    push1 = down[0]
    push2 = mm(down[1], push1)
    push3 = mm(down[2], push2)
    pushes = jnp.stack([eye, push1, push2, push3])
    weights = jnp.einsum("sqkp,spm->sqkm", cross, pushes, precision=highest)

    p = jnp.einsum("rk,skq->srq", root_coefficients, lifts, precision=highest)

    bit0 = me & 1
    bit1 = (me >> 1) & 1
    bit2 = (me >> 2) & 1
    got1 = swap_with(p, 1)
    pairs0 = ordered(bit0, p[0:1], got1[0:1])
    coef1 = p[1] + got1[1]
    part2 = p[2] + got1[2]
    part3 = p[3] + got1[3]
    got2 = swap_with(jnp.concatenate([pairs0, coef1[None], part2[None], part3[None]]), 2)
    quads0 = ordered(bit1, pairs0, got2[0:2])
    pairs1 = ordered(bit1, coef1[None], got2[2:3])
    coef2 = part2 + got2[3]
    part3 = part3 + got2[4]
    got3 = swap_with(jnp.concatenate([quads0, pairs1, coef2[None], part3[None]]), 4)
    octs0 = ordered(bit2, quads0, got3[0:4])
    quads1 = ordered(bit2, pairs1, got3[4:6])
    pairs2 = ordered(bit2, coef2[None], got3[6:7])
    coef3 = (part3 + got3[7])[None]

    node = 8
    to_ahead = jnp.concatenate([octs0[5:8], quads1[1:4], pairs2, coef3])
    to_behind = jnp.concatenate([octs0[0:3], quads1[0:3], pairs2, coef3])
    to_ahead, to_behind, first = lax.optimization_barrier((to_ahead, to_behind, first))
    ahead1 = receive_from(to_behind, node)
    behind1 = receive_from(to_ahead, -node)
    to_behind = jnp.concatenate([pairs2[0:1], coef3, ahead1[8:9]])
    to_ahead = jnp.concatenate([pairs2[1:2], coef3, behind1[8:9]])
    to_ahead, to_behind, second = lax.optimization_barrier((to_ahead, to_behind, second))
    ahead2 = receive_from(to_behind, 2 * node)
    behind2 = receive_from(to_ahead, -2 * node)
    ahead3 = ahead2[2:3]
    behind3 = behind2[2:3]

    window0 = jnp.concatenate([behind1[0:3], octs0, ahead1[0:3]])
    window1 = jnp.concatenate([behind1[3:6], quads1, ahead1[3:6]])
    window2 = jnp.concatenate([behind2[0:1], behind1[6:8], pairs2, ahead1[6:8], ahead2[0:1]])
    steps = jnp.array(partner_steps, dtype=jnp.int32) + 3
    chosen0 = jnp.take(window0, (me & 7) + steps, axis=0, mode="clip")
    chosen1 = jnp.take(window1, ((me >> 1) & 3) + steps, axis=0, mode="clip")
    chosen2 = jnp.take(window2, bit2 + steps, axis=0, mode="clip")
    chosen3 = jnp.concatenate([behind3, behind2[1:2], ahead2[1:2], ahead3])
    chosen = jnp.stack([chosen0, chosen1, chosen2, chosen3])
    return jnp.einsum("sqrk,sqkm->rm", chosen, weights, precision=highest), first, second


def local(
    sources,
    points,
    near_offsets,
    far_offsets,
    source_basis,
    target_basis,
    leaf_coupling,
    leaf_up,
    leaf_down,
    tree_up,
    tree_down,
    tree_coupling,
):
    leaf_count = near_offsets.shape[0]
    n = device_count()
    me = lax.axis_index("leaf") * lax.axis_size("grp") + lax.axis_index("grp")
    leaf_values = sources.reshape(RHS, leaf_count, CLUSTER)
    leaf_coefficients = jnp.einsum(
        "rla,lak->lrk",
        leaf_values,
        source_basis.reshape(leaf_count, CLUSTER, RANK),
        preferred_element_type=jnp.float32,
    )
    coef_rows = leaf_coefficients.reshape(leaf_count, RHS * RANK)

    packed = jnp.concatenate([sources.astype(jnp.float32), points], axis=0)
    width = NEAR_REACH * CLUSTER
    to_right = jnp.concatenate(
        [packed[:, -width:].reshape(-1), coef_rows[-FAR_REACH:].reshape(-1)]
    )
    to_left = jnp.concatenate([packed[:, :width].reshape(-1), coef_rows[:FAR_REACH].reshape(-1)])
    from_left = lax.ppermute(to_right, AXES, [(i, i + 1) for i in range(n - 1)])
    from_right = lax.ppermute(to_left, AXES, [(i + 1, i) for i in range(n - 1)])
    split = (RHS + 3) * width
    extended = jnp.concatenate(
        [
            from_left[:split].reshape(RHS + 3, width),
            packed,
            from_right[:split].reshape(RHS + 3, width),
        ],
        axis=1,
    ).reshape(RHS + 3, leaf_count + 2 * NEAR_REACH, CLUSTER)
    rimmed = jnp.concatenate(
        [
            from_left[split:].reshape(FAR_REACH, RHS * RANK),
            coef_rows,
            from_right[split:].reshape(FAR_REACH, RHS * RANK),
        ]
    )

    target_points = points.reshape(3, leaf_count, CLUSTER)
    near_sum = near_field_kernel(extended, target_points, near_offsets)

    far_index = jnp.arange(leaf_count, dtype=jnp.int32)[:, None] + FAR_REACH + far_offsets
    partner_blocks = jnp.take(rimmed, far_index, axis=0).reshape(leaf_count, FAR_BLOCKS, RHS, RANK)
    leaf_far = jnp.einsum(
        "lfrk,lfkq->lrq",
        partner_blocks,
        leaf_coupling.reshape(leaf_count, FAR_BLOCKS, RANK, RANK),
        precision=bf16_weights,
        preferred_element_type=jnp.float32,
    )
    root_coefficients = jnp.einsum(
        "lrk,lkq->rq",
        leaf_coefficients,
        leaf_up.reshape(leaf_count, RANK, RANK),
        precision=bf16_weights,
        preferred_element_type=jnp.float32,
    )
    downward, near_sum, leaf_far = tree_field(
        root_coefficients, tree_up, tree_down, tree_coupling, me, near_sum, leaf_far
    )
    from_root = jnp.einsum(
        "rk,lkq->lrq",
        downward,
        leaf_down.reshape(leaf_count, RANK, RANK),
        precision=bf16_weights,
        preferred_element_type=jnp.float32,
    )
    leaf_field = leaf_far + from_root
    far_out = jnp.einsum(
        "lrk,lka->lra",
        leaf_field,
        target_basis.reshape(leaf_count, RANK, CLUSTER),
        precision=bf16_weights,
        preferred_element_type=jnp.float32,
    )
    product = jnp.transpose(near_sum + far_out, (1, 0, 2))
    return product.reshape(RHS, leaf_count * CLUSTER)


def solution(mesh):
    placed = (
        P(None, AXES),
        P(None, AXES),
        P(AXES, None),
        P(AXES, None),
        P(AXES, None),
        P(AXES, None),
        P(AXES, None, None),
        P(AXES, None),
        P(AXES, None),
        P(AXES, None, None),
        P(AXES, None, None),
        P(AXES, None, None, None),
    )
    return jax.shard_map(
        local, mesh=mesh, in_specs=placed, out_specs=P(None, AXES), check_vma=False
    )
```

```python
import jax
import jax.numpy as jnp
from jax import lax
from jax.experimental import pallas as pl
from jax.experimental.pallas import tpu as pltpu
from jax.sharding import PartitionSpec as P

CLUSTER = 64
RANK = 32
RHS = 16
NEAR_REACH = 16
NEAR_BLOCKS = 6
FAR_REACH = 32
FAR_BLOCKS = 8
TOP_LEVELS = 3


amplitude = 0.15
length_scale = 1.0
nugget = 0.5
partner_steps = (-3, -2, 2, 3)
highest = lax.Precision.HIGHEST
bf16_weights = lax.Precision.HIGH
AXES = ("leaf", "grp")


def device_count():
    return lax.axis_size("leaf") * lax.axis_size("grp")


def swap_with(value, mask):
    n = device_count()
    return lax.ppermute(value, AXES, [(i, i ^ mask) for i in range(n)])


def receive_from(value, step):
    n = device_count()
    return lax.ppermute(value, AXES, [(s, s - step) for s in range(n) if 0 <= s - step < n])


def near_body(offsets_ref, table_ref, columns_ref, out_ref):
    leaf_count = out_ref.shape[0]
    rows = RHS + 3

    def one_leaf(i, carry):
        own = table_ref[i + NEAR_REACH]
        parts = []
        columns = jnp.transpose(columns_ref[i])[:CLUSTER]
        for pair in range(NEAR_BLOCKS // 2):
            first = table_ref[i + NEAR_REACH + offsets_ref[i, 2 * pair]]
            second = table_ref[i + NEAR_REACH + offsets_ref[i, 2 * pair + 1]]
            joined = jnp.concatenate([first, second], axis=1)
            squared = None
            for component in range(3):
                separation = joined[RHS + component : RHS + component + 1, :] - columns[:, component : component + 1]
                term = separation * separation
                squared = term if squared is None else squared + term
            kernel = (amplitude * jnp.exp(-jnp.sqrt(squared) / length_scale)).astype(jnp.bfloat16)
            values = joined[:RHS].astype(jnp.bfloat16)
            parts.append(
                lax.dot_general(
                    values, kernel, (((1,), (1,)), ((), ())), preferred_element_type=jnp.float32
                )
            )
        out_ref[i] = nugget * own[:RHS] + (parts[0] + parts[1] + parts[2])
        return carry

    lax.fori_loop(0, leaf_count, one_leaf, 0, unroll=True)


def near_field_kernel(extended, target_points, near_offsets):
    leaf_count = target_points.shape[1]
    by_leaf = jnp.transpose(extended, (1, 0, 2))
    table = by_leaf
    columns = jnp.pad(jnp.transpose(target_points, (1, 0, 2)), ((0, 0), (0, 5), (0, CLUSTER)))
    return pl.pallas_call(
        near_body,
        out_shape=jax.ShapeDtypeStruct((leaf_count, RHS, CLUSTER), jnp.float32),
        in_specs=[
            pl.BlockSpec(memory_space=pltpu.SMEM),
            pl.BlockSpec(memory_space=pltpu.VMEM),
            pl.BlockSpec(memory_space=pltpu.VMEM),
        ],
        out_specs=pl.BlockSpec(memory_space=pltpu.VMEM),
    )(near_offsets, table, columns)


def mm(a, b):
    return jnp.matmul(a, b, precision=highest, preferred_element_type=jnp.float32)


def ordered(bit, own, other):
    return jnp.where(bit == 0, jnp.concatenate([own, other]), jnp.concatenate([other, own]))


def tree_field(root_coefficients, tree_up, tree_down, tree_coupling, me, first, second):
    up = tree_up[0].astype(jnp.float32).reshape(TOP_LEVELS, RANK, RANK)
    down = tree_down[0].astype(jnp.float32).reshape(TOP_LEVELS, RANK, RANK)
    cross = tree_coupling[0].astype(jnp.float32).reshape(TOP_LEVELS + 1, 4, RANK, RANK)
    eye = jnp.eye(RANK, dtype=jnp.float32)
    lift1 = up[0]
    lift2 = mm(lift1, up[1])
    lift3 = mm(lift2, up[2])
    lifts = jnp.stack([eye, lift1, lift2, lift3])
    push1 = down[0]
    push2 = mm(down[1], push1)
    push3 = mm(down[2], push2)
    pushes = jnp.stack([eye, push1, push2, push3])
    weights = jnp.einsum("sqkp,spm->sqkm", cross, pushes, precision=highest)

    p = jnp.einsum("rk,skq->srq", root_coefficients, lifts, precision=highest)

    bit0 = me & 1
    bit1 = (me >> 1) & 1
    bit2 = (me >> 2) & 1
    got1 = swap_with(p, 1)
    pairs0 = ordered(bit0, p[0:1], got1[0:1])
    coef1 = p[1] + got1[1]
    part2 = p[2] + got1[2]
    part3 = p[3] + got1[3]
    got2 = swap_with(jnp.concatenate([pairs0, coef1[None], part2[None], part3[None]]), 2)
    quads0 = ordered(bit1, pairs0, got2[0:2])
    pairs1 = ordered(bit1, coef1[None], got2[2:3])
    coef2 = part2 + got2[3]
    part3 = part3 + got2[4]
    got3 = swap_with(jnp.concatenate([quads0, pairs1, coef2[None], part3[None]]), 4)
    octs0 = ordered(bit2, quads0, got3[0:4])
    quads1 = ordered(bit2, pairs1, got3[4:6])
    pairs2 = ordered(bit2, coef2[None], got3[6:7])
    coef3 = (part3 + got3[7])[None]

    node = 8
    to_ahead = jnp.concatenate([octs0[5:8], quads1[1:4], pairs2, coef3])
    to_behind = jnp.concatenate([octs0[0:3], quads1[0:3], pairs2, coef3])
    to_ahead, to_behind, first = lax.optimization_barrier((to_ahead, to_behind, first))
    ahead1 = receive_from(to_behind, node)
    behind1 = receive_from(to_ahead, -node)
    to_behind = jnp.concatenate([pairs2[0:1], coef3, ahead1[8:9]])
    to_ahead = jnp.concatenate([pairs2[1:2], coef3, behind1[8:9]])
    to_ahead, to_behind, second = lax.optimization_barrier((to_ahead, to_behind, second))
    ahead2 = receive_from(to_behind, 2 * node)
    behind2 = receive_from(to_ahead, -2 * node)
    ahead3 = ahead2[2:3]
    behind3 = behind2[2:3]

    window0 = jnp.concatenate([behind1[0:3], octs0, ahead1[0:3]])
    window1 = jnp.concatenate([behind1[3:6], quads1, ahead1[3:6]])
    window2 = jnp.concatenate([behind2[0:1], behind1[6:8], pairs2, ahead1[6:8], ahead2[0:1]])
    steps = jnp.array(partner_steps, dtype=jnp.int32) + 3
    chosen0 = jnp.take(window0, (me & 7) + steps, axis=0, mode="clip")
    chosen1 = jnp.take(window1, ((me >> 1) & 3) + steps, axis=0, mode="clip")
    chosen2 = jnp.take(window2, bit2 + steps, axis=0, mode="clip")
    chosen3 = jnp.concatenate([behind3, behind2[1:2], ahead2[1:2], ahead3])
    chosen = jnp.stack([chosen0, chosen1, chosen2, chosen3])
    return jnp.einsum("sqrk,sqkm->rm", chosen, weights, precision=highest), first, second


def local(
    sources,
    points,
    near_offsets,
    far_offsets,
    source_basis,
    target_basis,
    leaf_coupling,
    leaf_up,
    leaf_down,
    tree_up,
    tree_down,
    tree_coupling,
):
    leaf_count = near_offsets.shape[0]
    n = device_count()
    me = lax.axis_index("leaf") * lax.axis_size("grp") + lax.axis_index("grp")
    leaf_values = sources.reshape(RHS, leaf_count, CLUSTER)
    leaf_coefficients = jnp.einsum(
        "rla,lak->lrk",
        leaf_values,
        source_basis.reshape(leaf_count, CLUSTER, RANK),
        preferred_element_type=jnp.float32,
    )
    coef_rows = leaf_coefficients.reshape(leaf_count, RHS * RANK)

    packed = jnp.concatenate([sources.astype(jnp.float32), points], axis=0)
    width = NEAR_REACH * CLUSTER
    to_right = jnp.concatenate(
        [packed[:, -width:].reshape(-1), coef_rows[-FAR_REACH:].reshape(-1)]
    )
    to_left = jnp.concatenate([packed[:, :width].reshape(-1), coef_rows[:FAR_REACH].reshape(-1)])
    from_left = lax.ppermute(to_right, AXES, [(i, i + 1) for i in range(n - 1)])
    from_right = lax.ppermute(to_left, AXES, [(i + 1, i) for i in range(n - 1)])
    split = (RHS + 3) * width
    extended = jnp.concatenate(
        [
            from_left[:split].reshape(RHS + 3, width),
            packed,
            from_right[:split].reshape(RHS + 3, width),
        ],
        axis=1,
    ).reshape(RHS + 3, leaf_count + 2 * NEAR_REACH, CLUSTER)
    rimmed = jnp.concatenate(
        [
            from_left[split:].reshape(FAR_REACH, RHS * RANK),
            coef_rows,
            from_right[split:].reshape(FAR_REACH, RHS * RANK),
        ]
    )

    target_points = points.reshape(3, leaf_count, CLUSTER)
    near_sum = near_field_kernel(extended, target_points, near_offsets)

    far_index = jnp.arange(leaf_count, dtype=jnp.int32)[:, None] + FAR_REACH + far_offsets
    partner_blocks = jnp.take(rimmed, far_index, axis=0).reshape(leaf_count, FAR_BLOCKS, RHS, RANK)
    leaf_far = jnp.einsum(
        "lfrk,lfkq->lrq",
        partner_blocks,
        leaf_coupling.reshape(leaf_count, FAR_BLOCKS, RANK, RANK),
        precision=bf16_weights,
        preferred_element_type=jnp.float32,
    )
    root_coefficients = jnp.einsum(
        "lrk,lkq->rq",
        leaf_coefficients,
        leaf_up.reshape(leaf_count, RANK, RANK),
        precision=bf16_weights,
        preferred_element_type=jnp.float32,
    )
    downward, near_sum, leaf_far = tree_field(
        root_coefficients, tree_up, tree_down, tree_coupling, me, near_sum, leaf_far
    )
    from_root = jnp.einsum(
        "rk,lkq->lrq",
        downward,
        leaf_down.reshape(leaf_count, RANK, RANK),
        precision=bf16_weights,
        preferred_element_type=jnp.float32,
    )
    leaf_field = leaf_far + from_root
    far_out = jnp.einsum(
        "lrk,lka->lra",
        leaf_field,
        target_basis.reshape(leaf_count, RANK, CLUSTER),
        precision=bf16_weights,
        preferred_element_type=jnp.float32,
    )
    product = jnp.transpose(near_sum + far_out, (1, 0, 2))
    return product.reshape(RHS, leaf_count * CLUSTER)


def solution(mesh):
    placed = (
        P(None, AXES),
        P(None, AXES),
        P(AXES, None),
        P(AXES, None),
        P(AXES, None),
        P(AXES, None),
        P(AXES, None, None),
        P(AXES, None),
        P(AXES, None),
        P(AXES, None, None),
        P(AXES, None, None),
        P(AXES, None, None, None),
    )
    return jax.shard_map(
        local, mesh=mesh, in_specs=placed, out_specs=P(None, AXES), check_vma=False
    )
```

```python
import jax
import jax.numpy as jnp
from jax import lax
from jax.experimental import pallas as pl
from jax.experimental.pallas import tpu as pltpu
from jax.sharding import PartitionSpec as P

CLUSTER = 64
RANK = 32
RHS = 16
NEAR_REACH = 16
NEAR_BLOCKS = 6
FAR_REACH = 32
FAR_BLOCKS = 8
TOP_LEVELS = 3


amplitude = 0.15
length_scale = 1.0
nugget = 0.5
partner_steps = (-3, -2, 2, 3)
highest = lax.Precision.HIGHEST
bf16_weights = lax.Precision.HIGH
AXES = ("leaf", "grp")


def device_count():
    return lax.axis_size("leaf") * lax.axis_size("grp")


def swap_with(value, mask):
    n = device_count()
    return lax.ppermute(value, AXES, [(i, i ^ mask) for i in range(n)])


def receive_from(value, step):
    n = device_count()
    return lax.ppermute(value, AXES, [(s, s - step) for s in range(n) if 0 <= s - step < n])


def near_body(offsets_ref, table_ref, columns_ref, out_ref):
    leaf_count = out_ref.shape[0]
    rows = RHS + 3

    def one_leaf(i, carry):
        own = table_ref[i + NEAR_REACH]
        parts = []
        columns = jnp.transpose(columns_ref[i])[:CLUSTER]
        for pair in range(NEAR_BLOCKS // 2):
            first = table_ref[i + NEAR_REACH + offsets_ref[i, 2 * pair]]
            second = table_ref[i + NEAR_REACH + offsets_ref[i, 2 * pair + 1]]
            joined = jnp.concatenate([first, second], axis=1)
            squared = None
            for component in range(3):
                separation = joined[RHS + component : RHS + component + 1, :] - columns[:, component : component + 1]
                term = separation * separation
                squared = term if squared is None else squared + term
            kernel = (amplitude * jnp.exp(-jnp.sqrt(squared) / length_scale)).astype(jnp.bfloat16)
            values = joined[:RHS].astype(jnp.bfloat16)
            parts.append(
                lax.dot_general(
                    values, kernel, (((1,), (1,)), ((), ())), preferred_element_type=jnp.float32
                )
            )
        out_ref[i] = nugget * own[:RHS] + (parts[0] + parts[1] + parts[2])
        return carry

    lax.fori_loop(0, leaf_count, one_leaf, 0, unroll=True)


def near_field_kernel(extended, target_points, near_offsets):
    leaf_count = target_points.shape[1]
    by_leaf = jnp.transpose(extended, (1, 0, 2))
    table = by_leaf
    columns = jnp.pad(jnp.transpose(target_points, (1, 0, 2)), ((0, 0), (0, 5), (0, CLUSTER)))
    return pl.pallas_call(
        near_body,
        out_shape=jax.ShapeDtypeStruct((leaf_count, RHS, CLUSTER), jnp.float32),
        in_specs=[
            pl.BlockSpec(memory_space=pltpu.SMEM),
            pl.BlockSpec(memory_space=pltpu.VMEM),
            pl.BlockSpec(memory_space=pltpu.VMEM),
        ],
        out_specs=pl.BlockSpec(memory_space=pltpu.VMEM),
    )(near_offsets, table, columns)


def mm(a, b):
    return jnp.matmul(a, b, precision=highest, preferred_element_type=jnp.float32)


def ordered(bit, own, other):
    return jnp.where(bit == 0, jnp.concatenate([own, other]), jnp.concatenate([other, own]))


def tree_field(root_coefficients, tree_up, tree_down, tree_coupling, me, first, second):
    up = tree_up[0].astype(jnp.float32).reshape(TOP_LEVELS, RANK, RANK)
    down = tree_down[0].astype(jnp.float32).reshape(TOP_LEVELS, RANK, RANK)
    cross = tree_coupling[0].astype(jnp.float32).reshape(TOP_LEVELS + 1, 4, RANK, RANK)
    eye = jnp.eye(RANK, dtype=jnp.float32)
    lift1 = up[0]
    lift2 = mm(lift1, up[1])
    lift3 = mm(lift2, up[2])
    lifts = jnp.stack([eye, lift1, lift2, lift3])
    push1 = down[0]
    push2 = mm(down[1], push1)
    push3 = mm(down[2], push2)
    pushes = jnp.stack([eye, push1, push2, push3])
    weights = jnp.einsum("sqkp,spm->sqkm", cross, pushes, precision=highest)

    p = jnp.einsum("rk,skq->srq", root_coefficients, lifts, precision=highest)

    bit0 = me & 1
    bit1 = (me >> 1) & 1
    bit2 = (me >> 2) & 1
    got1 = swap_with(p, 1)
    pairs0 = ordered(bit0, p[0:1], got1[0:1])
    coef1 = p[1] + got1[1]
    part2 = p[2] + got1[2]
    part3 = p[3] + got1[3]
    got2 = swap_with(jnp.concatenate([pairs0, coef1[None], part2[None], part3[None]]), 2)
    quads0 = ordered(bit1, pairs0, got2[0:2])
    pairs1 = ordered(bit1, coef1[None], got2[2:3])
    coef2 = part2 + got2[3]
    part3 = part3 + got2[4]
    got3 = swap_with(jnp.concatenate([quads0, pairs1, coef2[None], part3[None]]), 4)
    octs0 = ordered(bit2, quads0, got3[0:4])
    quads1 = ordered(bit2, pairs1, got3[4:6])
    pairs2 = ordered(bit2, coef2[None], got3[6:7])
    coef3 = (part3 + got3[7])[None]

    node = 8
    to_ahead = jnp.concatenate([octs0[5:8], quads1[1:4], pairs2, coef3])
    to_behind = jnp.concatenate([octs0[0:3], quads1[0:3], pairs2, coef3])
    to_ahead, to_behind, first = lax.optimization_barrier((to_ahead, to_behind, first))
    ahead1 = receive_from(to_behind, node)
    behind1 = receive_from(to_ahead, -node)
    to_behind = jnp.concatenate([pairs2[0:1], coef3, ahead1[8:9]])
    to_ahead = jnp.concatenate([pairs2[1:2], coef3, behind1[8:9]])
    to_ahead, to_behind, second = lax.optimization_barrier((to_ahead, to_behind, second))
    ahead2 = receive_from(to_behind, 2 * node)
    behind2 = receive_from(to_ahead, -2 * node)
    ahead3 = ahead2[2:3]
    behind3 = behind2[2:3]

    window0 = jnp.concatenate([behind1[0:3], octs0, ahead1[0:3]])
    window1 = jnp.concatenate([behind1[3:6], quads1, ahead1[3:6]])
    window2 = jnp.concatenate([behind2[0:1], behind1[6:8], pairs2, ahead1[6:8], ahead2[0:1]])
    steps = jnp.array(partner_steps, dtype=jnp.int32) + 3
    chosen0 = jnp.take(window0, (me & 7) + steps, axis=0, mode="clip")
    chosen1 = jnp.take(window1, ((me >> 1) & 3) + steps, axis=0, mode="clip")
    chosen2 = jnp.take(window2, bit2 + steps, axis=0, mode="clip")
    chosen3 = jnp.concatenate([behind3, behind2[1:2], ahead2[1:2], ahead3])
    chosen = jnp.stack([chosen0, chosen1, chosen2, chosen3])
    return jnp.einsum("sqrk,sqkm->rm", chosen, weights, precision=highest), first, second


def local(
    sources,
    points,
    near_offsets,
    far_offsets,
    source_basis,
    target_basis,
    leaf_coupling,
    leaf_up,
    leaf_down,
    tree_up,
    tree_down,
    tree_coupling,
):
    leaf_count = near_offsets.shape[0]
    n = device_count()
    me = lax.axis_index("leaf") * lax.axis_size("grp") + lax.axis_index("grp")
    leaf_values = sources.reshape(RHS, leaf_count, CLUSTER)
    leaf_coefficients = jnp.einsum(
        "rla,lak->lrk",
        leaf_values,
        source_basis.reshape(leaf_count, CLUSTER, RANK),
        preferred_element_type=jnp.float32,
    )
    coef_rows = leaf_coefficients.reshape(leaf_count, RHS * RANK)

    packed = jnp.concatenate([sources.astype(jnp.float32), points], axis=0)
    width = NEAR_REACH * CLUSTER
    to_right = jnp.concatenate(
        [packed[:, -width:].reshape(-1), coef_rows[-FAR_REACH:].reshape(-1)]
    )
    to_left = jnp.concatenate([packed[:, :width].reshape(-1), coef_rows[:FAR_REACH].reshape(-1)])
    from_left = lax.ppermute(to_right, AXES, [(i, i + 1) for i in range(n - 1)])
    from_right = lax.ppermute(to_left, AXES, [(i + 1, i) for i in range(n - 1)])
    split = (RHS + 3) * width
    extended = jnp.concatenate(
        [
            from_left[:split].reshape(RHS + 3, width),
            packed,
            from_right[:split].reshape(RHS + 3, width),
        ],
        axis=1,
    ).reshape(RHS + 3, leaf_count + 2 * NEAR_REACH, CLUSTER)
    rimmed = jnp.concatenate(
        [
            from_left[split:].reshape(FAR_REACH, RHS * RANK),
            coef_rows,
            from_right[split:].reshape(FAR_REACH, RHS * RANK),
        ]
    )

    target_points = points.reshape(3, leaf_count, CLUSTER)
    near_sum = near_field_kernel(extended, target_points, near_offsets)

    far_index = jnp.arange(leaf_count, dtype=jnp.int32)[:, None] + FAR_REACH + far_offsets
    partner_blocks = jnp.take(rimmed, far_index, axis=0, mode="clip").reshape(leaf_count, FAR_BLOCKS, RHS, RANK)
    leaf_far = jnp.einsum(
        "lfrk,lfkq->lrq",
        partner_blocks,
        leaf_coupling.reshape(leaf_count, FAR_BLOCKS, RANK, RANK),
        precision=bf16_weights,
        preferred_element_type=jnp.float32,
    )
    root_coefficients = jnp.einsum(
        "lrk,lkq->rq",
        leaf_coefficients,
        leaf_up.reshape(leaf_count, RANK, RANK),
        precision=bf16_weights,
        preferred_element_type=jnp.float32,
    )
    downward, near_sum, leaf_far = tree_field(
        root_coefficients, tree_up, tree_down, tree_coupling, me, near_sum, leaf_far
    )
    from_root = jnp.einsum(
        "rk,lkq->lrq",
        downward,
        leaf_down.reshape(leaf_count, RANK, RANK),
        precision=bf16_weights,
        preferred_element_type=jnp.float32,
    )
    leaf_field = leaf_far + from_root
    far_out = jnp.einsum(
        "lrk,lka->lra",
        leaf_field,
        target_basis.reshape(leaf_count, RANK, CLUSTER),
        precision=bf16_weights,
        preferred_element_type=jnp.float32,
    )
    product = jnp.transpose(near_sum + far_out, (1, 0, 2))
    return product.reshape(RHS, leaf_count * CLUSTER)


def solution(mesh):
    placed = (
        P(None, AXES),
        P(None, AXES),
        P(AXES, None),
        P(AXES, None),
        P(AXES, None),
        P(AXES, None),
        P(AXES, None, None),
        P(AXES, None),
        P(AXES, None),
        P(AXES, None, None),
        P(AXES, None, None),
        P(AXES, None, None, None),
    )
    return jax.shard_map(
        local, mesh=mesh, in_specs=placed, out_specs=P(None, AXES), check_vma=False
    )
```
